256 devices in a mesh: space: 128 (over z, y, x), vel: 2 (over core).
Axes of the slice: x: 4, y: 4, z: 8, core: 2. Of those that a mesh axis runs over, the one named last changes fastest.
Arguments:
- adjoint: bfloat16 [4096, 512, 256], P('vel', 'space'), may hold values from -15 to 15
- collision: float32 [512, 256], P('space'), may hold values from 0.5 to 2
- solid: int32 [512, 256], P('space'), may hold values 0 or 1
- codes: int32 [512, 256], P('space'), may hold values from 0 to 3
Outputs:
- corrected: bfloat16 [4096, 512, 256], P('vel', 'space')
- synthetic: float32 [13, 512, 256], P(None, 'space')
The draws below stay inside these ranges and needn't reach their ends.
All inputs are finite; a program needn't handle non-finite values. No bound on the sum of `solid` on one device may be relied on, other than what follows from the above.
Results may differ from the reference program's by a relative error of at most 0.0053.
Values may be sent and summed in bfloat16 or wider, within the bound.
No kernel may reach another device: no remote copies, remote signals or barrier semaphores. Data moves between devices by JAX's collectives and lax.ppermute only.
A program may use at most 128 MiB of HBM per device.

```python
import math
import jax
import jax.numpy as jnp
from jax import lax

NV1 = 16
NM = 13
CX = 4
NY = 16
NZ = 16
SWEEPS = 3
NX = 512


def draw_adjoint(key, part):
    shape = (NV1 ** 3, NX, NY * NZ)
    blocks = NX // CX
    levels = jnp.exp(jax.random.uniform(jax.random.fold_in(key, 7), (blocks,), jnp.float32, -1.1, 1.1))
    rows = jnp.arange(NX, dtype=jnp.int32)
    halves = jnp.where(rows >= NX // 2, 2.0, 1.0).astype(jnp.float32)
    amplitude = (jnp.repeat(levels, CX, total_repeat_length=NX) * halves)[None, :, None]
    value_key = jax.random.fold_in(key, 11)
    values = jnp.clip(jax.random.normal(value_key, shape, jnp.float32), -2.4, 2.4) * amplitude
    return values.astype(jnp.bfloat16)


def set_ends(array, own_key, least, top_value):
    longest = array.shape.index(max(array.shape))
    spots = []
    for shift in (0, 1):
        where = [jax.random.randint(jax.random.fold_in(own_key, axis), (), 0, length) for axis, length in enumerate(array.shape)]
        where[longest] = (where[longest] + shift) % array.shape[longest]
        spots.append(tuple(where))
    return array.at[spots[0]].set(least).at[spots[1]].set(top_value)


def steps_of(key, extent, split, least, high):
    loudness = 1.0
    for axis_at, blocks in split:
        draws = jax.random.uniform(jax.random.fold_in(jax.random.fold_in(key, 6), axis_at), (blocks,), jnp.float32, least / len(split), high / len(split))
        loudness = loudness * jnp.repeat(jnp.exp(draws), extent[axis_at] // blocks).reshape((-1,) + (1,) * (len(extent) - 1 - axis_at))
    return loudness


def setup_inputs(seed: int = 0) -> dict:
    splits = jax.random.split(jax.random.key(seed), 5)
    return {
        "adjoint": draw_adjoint(jax.random.fold_in(splits[4], 71), 0),
        "collision": jnp.clip(jnp.exp(math.log(2.0) - 1.3862944 * jax.random.uniform(splits[1], (NX, NY * NZ), jnp.float32) ** steps_of(splits[1], (NX, NY * NZ), ((0, 128),), -0.2, 0.2)), 0.5, 2.0),
        "solid": set_ends((jax.random.randint(splits[2], (NX, NY * NZ), 0, 8) < 1).astype(jnp.int32), jax.random.fold_in(splits[2], 1), 0, 1),
        "codes": set_ends(jax.random.randint(splits[3], (NX, NY * NZ), 0, 4), jax.random.fold_in(splits[3], 1), 0, 3).astype(jnp.int32),
    }


TIME_STEP = 0.06

def velocity_axes(start, count):
    index = start + jnp.arange(count, dtype=jnp.int32)
    spacing = 9.0 / NV1
    centre = (NV1 - 1) / 2.0
    along_x = ((index % NV1).astype(jnp.float32) - centre) * spacing
    along_z = ((index // NV1 % NV1).astype(jnp.float32) - centre) * spacing
    along_y = ((index // (NV1 * NV1)).astype(jnp.float32) - centre) * spacing
    return (along_x, along_y, along_z)

def tables(start, count):
    along_x, along_y, along_z = velocity_axes(start, count)
    speed = along_x * along_x + along_y * along_y + along_z * along_z
    unity = jnp.ones_like(along_x)
    basis = jnp.stack([unity, along_x, along_y, along_z, (speed - 3.0) / math.sqrt(6.0), along_x * along_y, along_x * along_z, along_y * along_z, (along_x * along_x - along_y * along_y) / math.sqrt(2.0), (along_x * along_x + along_y * along_y - 2.0 * along_z * along_z) / math.sqrt(6.0), along_x * (speed - 5.0) / math.sqrt(10.0), along_y * (speed - 5.0) / math.sqrt(10.0), along_z * (speed - 5.0) / math.sqrt(10.0)])
    every_x, every_y, every_z = velocity_axes(0, NV1 ** 3)
    total = jnp.sum(jnp.exp(-0.5 * (every_x * every_x + every_y * every_y + every_z * every_z)))
    weigh = (basis * jnp.exp(-0.5 * speed) / total).astype(jnp.bfloat16)
    lift = jnp.transpose(0.1 * basis * jnp.exp(-0.25 * speed)).astype(jnp.bfloat16)
    return (along_x, along_y, along_z, weigh, lift)

def wall_level(codes):
    return 0.5 * (codes == 1).astype(jnp.float32) + 1.5 * (codes == 2).astype(jnp.float32) + 4.0 * (codes == 3).astype(jnp.float32)

def reference(adjoint, collision, solid, codes):
    count_all = NV1 ** 3
    cells = NX * NY * NZ
    fluid = (1 - solid).astype(jnp.float32).reshape(NX, NY, NZ)
    rates = collision.reshape(NX, NY, NZ)
    along_x, along_y, along_z, weigh, lift = tables(0, count_all)
    group = NV1 * NV1
    blocks = count_all // group

    def advance(index):
        start = index * group
        piece = lax.dynamic_slice_in_dim(adjoint, start, group, 0).astype(jnp.float32).reshape(group, NX, NY, NZ)
        speed_x = lax.dynamic_slice_in_dim(along_x, start, group, 0)[:, None, None, None]
        speed_y = lax.dynamic_slice_in_dim(along_y, start, group, 0)[:, None, None, None]
        speed_z = lax.dynamic_slice_in_dim(along_z, start, group, 0)[:, None, None, None]
        padded = jnp.pad(piece, ((0, 0), (1, 1), (1, 1), (1, 1)))
        core = padded[:, 1:-1, 1:-1, 1:-1]
        term_x = jnp.maximum(speed_x, 0.0) * (padded[:, 2:, 1:-1, 1:-1] - core) + jnp.minimum(speed_x, 0.0) * (core - padded[:, :-2, 1:-1, 1:-1])
        term_y = jnp.maximum(speed_y, 0.0) * (padded[:, 1:-1, 2:, 1:-1] - core) + jnp.minimum(speed_y, 0.0) * (core - padded[:, 1:-1, :-2, 1:-1])
        term_z = jnp.maximum(speed_z, 0.0) * (padded[:, 1:-1, 1:-1, 2:] - core) + jnp.minimum(speed_z, 0.0) * (core - padded[:, 1:-1, 1:-1, :-2])
        advect = term_x + term_y + term_z
        starred = (fluid * (piece + TIME_STEP * (advect - rates * piece))).astype(jnp.bfloat16)
        weights = lax.dynamic_slice_in_dim(weigh, start, group, 1)
        partial_value = jnp.dot(weights, starred.reshape(group, cells), preferred_element_type=jnp.float32)
        return (starred.reshape(group, cells), partial_value)
    starred_all, partials = lax.map(advance, jnp.arange(blocks, dtype=jnp.int32))
    moments = lax.optimization_barrier(jnp.sum(partials, axis=0)).reshape(NM, NX, NY, NZ)
    scale = lax.rsqrt(jnp.sum(moments[0] * moments[0]) / cells + 1e-06)
    inverse = fluid / (rates + wall_level(codes).reshape(NX, NY, NZ) + 6.0)
    source = rates * moments
    fields = moments * fluid
    for sweep in range(SWEEPS):
        padded = jnp.pad(fields, ((0, 0), (1, 1), (1, 1), (1, 1)))
        beside_all = padded[:, 2:, 1:-1, 1:-1] + padded[:, :-2, 1:-1, 1:-1] + padded[:, 1:-1, 2:, 1:-1] + padded[:, 1:-1, :-2, 1:-1] + padded[:, 1:-1, 1:-1, 2:] + padded[:, 1:-1, 1:-1, :-2]
        fields = inverse * (source + beside_all)
    delta = ((fields - moments) * scale).astype(jnp.bfloat16).reshape(NM, cells)
    fluid_flat = fluid.reshape(1, cells)

    def correct(index):
        lifts = lax.dynamic_slice_in_dim(lift, index * group, group, 0)
        added = jnp.dot(lifts, delta, preferred_element_type=jnp.float32)
        return (fluid_flat * (starred_all[index] + added)).astype(jnp.bfloat16)
    corrected = lax.map(correct, jnp.arange(blocks, dtype=jnp.int32)).reshape(count_all, NX, NY * NZ)
    return (corrected, (fields * scale).reshape(NM, NX, NY * NZ))
```

```python
import math

import jax
import jax.numpy as jnp
from jax import lax
from jax.sharding import PartitionSpec as P

NV1 = 16
NM = 13
NY = 16
NZ = 16
SWEEPS = 3


TIME_STEP = 0.06


def with_halo(cells, sides, width):
    for axis, dim in sides:
        count = lax.axis_size(axis)
        ends = count - 1
        head = lax.slice_in_dim(cells, 0, width, axis=dim)
        tail = lax.slice_in_dim(cells, cells.shape[dim] - width, cells.shape[dim], axis=dim)
        cells = jnp.concatenate(
            [
                lax.ppermute(tail, axis, [(i, (i + 1) % count) for i in range(ends)]),
                cells,
                lax.ppermute(head, axis, [((i + 1) % count, i) for i in range(ends)]),
            ],
            axis=dim,
        )
    return cells


def velocity_axes(start, count):
    index = start + jnp.arange(count, dtype=jnp.int32)
    spacing = 9.0 / NV1
    centre = (NV1 - 1) / 2.0
    along_x = ((index % NV1).astype(jnp.float32) - centre) * spacing
    along_z = ((index // NV1 % NV1).astype(jnp.float32) - centre) * spacing
    along_y = ((index // (NV1 * NV1)).astype(jnp.float32) - centre) * spacing
    return (along_x, along_y, along_z)


def tables(start, count):
    along_x, along_y, along_z = velocity_axes(start, count)
    speed = along_x * along_x + along_y * along_y + along_z * along_z
    unity = jnp.ones_like(along_x)
    basis = jnp.stack(
        [
            unity,
            along_x,
            along_y,
            along_z,
            (speed - 3.0) / math.sqrt(6.0),
            along_x * along_y,
            along_x * along_z,
            along_y * along_z,
            (along_x * along_x - along_y * along_y) / math.sqrt(2.0),
            (along_x * along_x + along_y * along_y - 2.0 * along_z * along_z) / math.sqrt(6.0),
            along_x * (speed - 5.0) / math.sqrt(10.0),
            along_y * (speed - 5.0) / math.sqrt(10.0),
            along_z * (speed - 5.0) / math.sqrt(10.0),
        ]
    )
    every_x, every_y, every_z = velocity_axes(0, NV1**3)
    total = jnp.sum(jnp.exp(-0.5 * (every_x * every_x + every_y * every_y + every_z * every_z)))
    weigh = (basis * jnp.exp(-0.5 * speed) / total).astype(jnp.bfloat16)
    lift = jnp.transpose(0.1 * basis * jnp.exp(-0.25 * speed)).astype(jnp.bfloat16)
    return (along_x, along_y, along_z, weigh, lift)


def wall_level(codes):
    return (
        0.5 * (codes == 1).astype(jnp.float32)
        + 1.5 * (codes == 2).astype(jnp.float32)
        + 4.0 * (codes == 3).astype(jnp.float32)
    )


def plane_around(fields):
    count, rows, plane = fields.shape
    cube = fields.reshape(count, rows, NY, NZ)
    padded = jnp.pad(cube, ((0, 0), (0, 0), (1, 1), (1, 1)))
    summed = (
        padded[:, :, 2:, 1:-1]
        + padded[:, :, :-2, 1:-1]
        + padded[:, :, 1:-1, 2:]
        + padded[:, :, 1:-1, :-2]
    )
    return summed.reshape(count, rows, plane)


def sweep_each(fields, source, inverse):
    widened = with_halo(fields.astype(jnp.bfloat16), (("space", 1),), 1).astype(fields.dtype)
    beside_all = widened[:, 2:] + widened[:, :-2] + plane_around(fields)
    return inverse * (source + beside_all)


def on_device(adjoint, collision, solid, codes):
    local_vel, width, plane = adjoint.shape
    start = lax.axis_index("vel") * local_vel
    speed_x, speed_y, speed_z, weigh, lift = tables(start, local_vel)
    half = NV1 // 2
    groups = local_vel // NV1
    grid = adjoint.reshape(groups, NV1, width, plane)
    widened = with_halo(adjoint, (("space", 1),), 1).reshape(groups, NV1, width + 2, plane)
    left_rim = widened[:, :half, 0]
    right_rim = widened[:, half:, width + 1]
    lower = grid[:, :half].astype(jnp.float32)
    upper = grid[:, half:].astype(jnp.float32)
    before = jnp.concatenate([left_rim[:, :, None].astype(jnp.float32), lower[:, :, :-1]], axis=2)
    after = jnp.concatenate([upper[:, :, 1:], right_rim[:, :, None].astype(jnp.float32)], axis=2)
    shaped_x = speed_x.reshape(groups, NV1, 1, 1)
    term_x = jnp.concatenate(
        [shaped_x[:, :half] * (lower - before), shaped_x[:, half:] * (after - upper)], axis=1
    )
    term_x = term_x.reshape(local_vel, width, plane)
    flat = adjoint.astype(jnp.float32)
    cube = flat.reshape(local_vel, width, NY, NZ)
    padded = jnp.pad(cube, ((0, 0), (0, 0), (1, 1), (1, 1)))
    shaped_y = speed_y[:, None, None, None]
    shaped_z = speed_z[:, None, None, None]
    term_y = jnp.maximum(shaped_y, 0.0) * (padded[:, :, 2:, 1:-1] - cube) + jnp.minimum(
        shaped_y, 0.0
    ) * (cube - padded[:, :, :-2, 1:-1])
    term_z = jnp.maximum(shaped_z, 0.0) * (padded[:, :, 1:-1, 2:] - cube) + jnp.minimum(
        shaped_z, 0.0
    ) * (cube - padded[:, :, 1:-1, :-2])
    advect = (
        term_x + term_y.reshape(local_vel, width, plane) + term_z.reshape(local_vel, width, plane)
    )
    fluid = (1 - solid).astype(jnp.float32)
    starred = (fluid[None] * (flat + TIME_STEP * (advect - collision[None] * flat))).astype(
        jnp.bfloat16
    )
    starred_flat = starred.reshape(local_vel, width * plane)
    partial_value = jnp.dot(weigh, starred_flat, preferred_element_type=jnp.float32)
    moments = lax.psum(partial_value, "vel").reshape(NM, width, plane)
    cells_all = width * lax.axis_size("space") * plane
    own = jnp.sum(moments[0] * moments[0])
    own = jnp.where(lax.axis_index("vel") == 0, own, 0.0)
    squares = lax.psum(own, ("space", "vel"))
    scale = lax.rsqrt(squares / cells_all + 1e-06)
    inverse = fluid / (collision + wall_level(codes) + 6.0)
    source = collision[None] * moments
    fields = moments * fluid[None]
    for sweep in range(SWEEPS):
        fields = sweep_each(fields, source, inverse[None])
    delta = ((fields - moments) * scale).astype(jnp.bfloat16).reshape(NM, width * plane)
    added = jnp.dot(lift, delta, preferred_element_type=jnp.float32)
    corrected = (fluid.reshape(1, width * plane) * (starred_flat + added)).astype(jnp.bfloat16)
    return (corrected.reshape(local_vel, width, plane), fields * scale)


def solution(mesh):
    return jax.shard_map(
        on_device,
        mesh=mesh,
        in_specs=(P("vel", "space", None), P("space", None), P("space", None), P("space", None)),
        out_specs=(P("vel", "space", None), P(None, "space", None)),
        check_vma=False,
    )
```

```python
import math

import jax
import jax.numpy as jnp
from jax import lax
from jax.sharding import PartitionSpec as P

NV1 = 16
NM = 13
NY = 16
NZ = 16
SWEEPS = 3


TIME_STEP = 0.06


def with_halo(cells, sides, width):
    for axis, dim in sides:
        count = lax.axis_size(axis)
        ends = count - 1
        head = lax.slice_in_dim(cells, 0, width, axis=dim)
        tail = lax.slice_in_dim(cells, cells.shape[dim] - width, cells.shape[dim], axis=dim)
        cells = jnp.concatenate(
            [
                lax.ppermute(tail, axis, [(i, (i + 1) % count) for i in range(ends)]),
                cells,
                lax.ppermute(head, axis, [((i + 1) % count, i) for i in range(ends)]),
            ],
            axis=dim,
        )
    return cells


def exchange_sum(value, axis):
    count = lax.axis_size(axis)
    if count & (count - 1):
        return lax.psum(value, axis)
    step = 1
    while step < count:
        value = value + lax.ppermute(value, axis, [(i, i ^ step) for i in range(count)])
        step *= 2
    return value


def velocity_axes(start, count):
    index = start + jnp.arange(count, dtype=jnp.int32)
    spacing = 9.0 / NV1
    centre = (NV1 - 1) / 2.0
    along_x = ((index % NV1).astype(jnp.float32) - centre) * spacing
    along_z = ((index // NV1 % NV1).astype(jnp.float32) - centre) * spacing
    along_y = ((index // (NV1 * NV1)).astype(jnp.float32) - centre) * spacing
    return (along_x, along_y, along_z)


def tables(start, count):
    along_x, along_y, along_z = velocity_axes(start, count)
    speed = along_x * along_x + along_y * along_y + along_z * along_z
    unity = jnp.ones_like(along_x)
    basis = jnp.stack(
        [
            unity,
            along_x,
            along_y,
            along_z,
            (speed - 3.0) / math.sqrt(6.0),
            along_x * along_y,
            along_x * along_z,
            along_y * along_z,
            (along_x * along_x - along_y * along_y) / math.sqrt(2.0),
            (along_x * along_x + along_y * along_y - 2.0 * along_z * along_z) / math.sqrt(6.0),
            along_x * (speed - 5.0) / math.sqrt(10.0),
            along_y * (speed - 5.0) / math.sqrt(10.0),
            along_z * (speed - 5.0) / math.sqrt(10.0),
        ]
    )
    every_x, every_y, every_z = velocity_axes(0, NV1**3)
    total = jnp.sum(jnp.exp(-0.5 * (every_x * every_x + every_y * every_y + every_z * every_z)))
    weigh = (basis * jnp.exp(-0.5 * speed) / total).astype(jnp.bfloat16)
    lift = jnp.transpose(0.1 * basis * jnp.exp(-0.25 * speed)).astype(jnp.bfloat16)
    return (along_x, along_y, along_z, weigh, lift)


def wall_level(codes):
    return (
        0.5 * (codes == 1).astype(jnp.float32)
        + 1.5 * (codes == 2).astype(jnp.float32)
        + 4.0 * (codes == 3).astype(jnp.float32)
    )


def plane_around(fields):
    count, rows, plane = fields.shape
    cube = fields.reshape(count, rows, NY, NZ)
    padded = jnp.pad(cube, ((0, 0), (0, 0), (1, 1), (1, 1)))
    summed = (
        padded[:, :, 2:, 1:-1]
        + padded[:, :, :-2, 1:-1]
        + padded[:, :, 1:-1, 2:]
        + padded[:, :, 1:-1, :-2]
    )
    return summed.reshape(count, rows, plane)


def sweep_each(fields, source, inverse):
    widened = with_halo(fields.astype(jnp.bfloat16), (("space", 1),), 1).astype(fields.dtype)
    beside_all = widened[:, 2:] + widened[:, :-2] + plane_around(fields)
    return inverse * (source + beside_all)


def on_device(adjoint, collision, solid, codes):
    local_vel, width, plane = adjoint.shape
    start = lax.axis_index("vel") * local_vel
    speed_x, speed_y, speed_z, weigh, lift = tables(start, local_vel)
    half = NV1 // 2
    groups = local_vel // NV1
    grid = adjoint.reshape(groups, NV1, width, plane)
    widened = with_halo(adjoint, (("space", 1),), 1).reshape(groups, NV1, width + 2, plane)
    left_rim = widened[:, :half, 0]
    right_rim = widened[:, half:, width + 1]
    lower = grid[:, :half].astype(jnp.float32)
    upper = grid[:, half:].astype(jnp.float32)
    before = jnp.concatenate([left_rim[:, :, None].astype(jnp.float32), lower[:, :, :-1]], axis=2)
    after = jnp.concatenate([upper[:, :, 1:], right_rim[:, :, None].astype(jnp.float32)], axis=2)
    shaped_x = speed_x.reshape(groups, NV1, 1, 1)
    term_x = jnp.concatenate(
        [shaped_x[:, :half] * (lower - before), shaped_x[:, half:] * (after - upper)], axis=1
    )
    term_x = term_x.reshape(local_vel, width, plane)
    flat = adjoint.astype(jnp.float32)
    cube = flat.reshape(local_vel, width, NY, NZ)
    padded = jnp.pad(cube, ((0, 0), (0, 0), (1, 1), (1, 1)))
    shaped_y = speed_y[:, None, None, None]
    shaped_z = speed_z[:, None, None, None]
    term_y = jnp.maximum(shaped_y, 0.0) * (padded[:, :, 2:, 1:-1] - cube) + jnp.minimum(
        shaped_y, 0.0
    ) * (cube - padded[:, :, :-2, 1:-1])
    term_z = jnp.maximum(shaped_z, 0.0) * (padded[:, :, 1:-1, 2:] - cube) + jnp.minimum(
        shaped_z, 0.0
    ) * (cube - padded[:, :, 1:-1, :-2])
    advect = (
        term_x + term_y.reshape(local_vel, width, plane) + term_z.reshape(local_vel, width, plane)
    )
    fluid = (1 - solid).astype(jnp.float32)
    starred = (fluid[None] * (flat + TIME_STEP * (advect - collision[None] * flat))).astype(
        jnp.bfloat16
    )
    starred_flat = starred.reshape(local_vel, width * plane)
    partial_value = jnp.dot(weigh, starred_flat, preferred_element_type=jnp.float32)
    moments = lax.psum(partial_value, "vel").reshape(NM, width, plane)
    cells_all = width * lax.axis_size("space") * plane
    squares = exchange_sum(jnp.sum(moments[0] * moments[0]), "space")
    scale = lax.rsqrt(squares / cells_all + 1e-06)
    inverse = fluid / (collision + wall_level(codes) + 6.0)
    source = collision[None] * moments
    fields = moments * fluid[None]
    for sweep in range(SWEEPS):
        fields = sweep_each(fields, source, inverse[None])
    delta = ((fields - moments) * scale).astype(jnp.bfloat16).reshape(NM, width * plane)
    added = jnp.dot(lift, delta, preferred_element_type=jnp.float32)
    corrected = (fluid.reshape(1, width * plane) * (starred_flat + added)).astype(jnp.bfloat16)
    return (corrected.reshape(local_vel, width, plane), fields * scale)


def solution(mesh):
    return jax.shard_map(
        on_device,
        mesh=mesh,
        in_specs=(P("vel", "space", None), P("space", None), P("space", None), P("space", None)),
        out_specs=(P("vel", "space", None), P(None, "space", None)),
        check_vma=False,
    )
```

```python
import math

import jax
import jax.numpy as jnp
from jax import lax
from jax.sharding import PartitionSpec as P
from jax.experimental import pallas as pl
from jax.experimental.pallas import tpu as pltpu

NV1 = 16
NM = 13
NY = 16
NZ = 16
SWEEPS = 3


TIME_STEP = 0.06
PLANE = NY * NZ


def with_halo(cells, sides, width):
    for axis, dim in sides:
        count = lax.axis_size(axis)
        ends = count - 1
        head = lax.slice_in_dim(cells, 0, width, axis=dim)
        tail = lax.slice_in_dim(cells, cells.shape[dim] - width, cells.shape[dim], axis=dim)
        cells = jnp.concatenate(
            [
                lax.ppermute(tail, axis, [(i, (i + 1) % count) for i in range(ends)]),
                cells,
                lax.ppermute(head, axis, [((i + 1) % count, i) for i in range(ends)]),
            ],
            axis=dim,
        )
    return cells


def exchange_sum(value, axis):
    count = lax.axis_size(axis)
    if count & (count - 1):
        return lax.psum(value, axis)
    step = 1
    while step < count:
        value = value + lax.ppermute(value, axis, [(i, i ^ step) for i in range(count)])
        step *= 2
    return value


def velocity_axes(start, count):
    index = start + jnp.arange(count, dtype=jnp.int32)
    spacing = 9.0 / NV1
    centre = (NV1 - 1) / 2.0
    along_x = ((index % NV1).astype(jnp.float32) - centre) * spacing
    along_z = ((index // NV1 % NV1).astype(jnp.float32) - centre) * spacing
    along_y = ((index // (NV1 * NV1)).astype(jnp.float32) - centre) * spacing
    return (along_x, along_y, along_z)


def tables(start, count):
    along_x, along_y, along_z = velocity_axes(start, count)
    speed = along_x * along_x + along_y * along_y + along_z * along_z
    unity = jnp.ones_like(along_x)
    basis = jnp.stack(
        [
            unity,
            along_x,
            along_y,
            along_z,
            (speed - 3.0) / math.sqrt(6.0),
            along_x * along_y,
            along_x * along_z,
            along_y * along_z,
            (along_x * along_x - along_y * along_y) / math.sqrt(2.0),
            (along_x * along_x + along_y * along_y - 2.0 * along_z * along_z) / math.sqrt(6.0),
            along_x * (speed - 5.0) / math.sqrt(10.0),
            along_y * (speed - 5.0) / math.sqrt(10.0),
            along_z * (speed - 5.0) / math.sqrt(10.0),
        ]
    )
    every_x, every_y, every_z = velocity_axes(0, NV1**3)
    total = jnp.sum(jnp.exp(-0.5 * (every_x * every_x + every_y * every_y + every_z * every_z)))
    weigh = (basis * jnp.exp(-0.5 * speed) / total).astype(jnp.bfloat16)
    lift = jnp.transpose(0.1 * basis * jnp.exp(-0.25 * speed)).astype(jnp.bfloat16)
    return (along_x, along_y, along_z, weigh, lift)


def wall_level(codes):
    return (
        0.5 * (codes == 1).astype(jnp.float32)
        + 1.5 * (codes == 2).astype(jnp.float32)
        + 4.0 * (codes == 3).astype(jnp.float32)
    )


def plane_around(fields):
    count, rows, plane = fields.shape
    cube = fields.reshape(count, rows, NY, NZ)
    padded = jnp.pad(cube, ((0, 0), (0, 0), (1, 1), (1, 1)))
    summed = (
        padded[:, :, 2:, 1:-1]
        + padded[:, :, :-2, 1:-1]
        + padded[:, :, 1:-1, 2:]
        + padded[:, :, 1:-1, :-2]
    )
    return summed.reshape(count, rows, plane)


def sweep_each(fields, source, inverse):
    widened = with_halo(fields.astype(jnp.bfloat16), (("space", 1),), 1).astype(fields.dtype)
    beside_all = widened[:, 2:] + widened[:, :-2] + plane_around(fields)
    return inverse * (source + beside_all)


def advance_kernel(adj_ref, left_ref, right_ref, cx_ref, cy_ref, cz_ref, coll_ref, fluid_ref, weigh_ref,
                   star_ref, part_ref):
    step = pl.program_id(0)
    g = adj_ref[...].astype(jnp.float32)
    rows, lanes = g.shape
    cx = cx_ref[...]
    cy = cy_ref[...]
    cz = cz_ref[...]
    left = left_ref[...].astype(jnp.float32)
    right = right_ref[...].astype(jnp.float32)
    after = jnp.concatenate([g[:, PLANE:], right], axis=1)
    before = jnp.concatenate([left, g[:, : lanes - PLANE]], axis=1)
    lane = lax.broadcasted_iota(jnp.int32, (1, lanes), 1)
    zpos = lane % NZ
    ypos = (lane // NZ) % (PLANE // NZ)
    y_next = jnp.where(ypos == PLANE // NZ - 1, 0.0, pltpu.roll(g, lanes - NZ, 1))
    y_prev = jnp.where(ypos == 0, 0.0, pltpu.roll(g, NZ, 1))
    z_next = jnp.where(zpos == NZ - 1, 0.0, pltpu.roll(g, lanes - 1, 1))
    z_prev = jnp.where(zpos == 0, 0.0, pltpu.roll(g, 1, 1))
    term_x = jnp.maximum(cx, 0.0) * (after - g) + jnp.minimum(cx, 0.0) * (g - before)
    term_y = jnp.maximum(cy, 0.0) * (y_next - g) + jnp.minimum(cy, 0.0) * (g - y_prev)
    term_z = jnp.maximum(cz, 0.0) * (z_next - g) + jnp.minimum(cz, 0.0) * (g - z_prev)
    advect = term_x + term_y + term_z
    starred = (fluid_ref[...] * (g + TIME_STEP * (advect - coll_ref[...] * g))).astype(jnp.bfloat16)
    star_ref[...] = starred
    partial = jnp.dot(weigh_ref[...], starred, preferred_element_type=jnp.float32)

    @pl.when(step == 0)
    def _():
        part_ref[...] = partial

    @pl.when(step > 0)
    def _():
        part_ref[...] += partial


def advance(adj, left, right, cx, cy, cz, coll, fluid, weigh, block=256):
    nv, lanes = adj.shape
    nm = weigh.shape[0]
    grid = (nv // block,)
    row = lambda i: (i, 0)
    fixed = lambda i: (0, 0)
    return pl.pallas_call(
        advance_kernel,
        grid=grid,
        in_specs=[
            pl.BlockSpec((block, lanes), row),
            pl.BlockSpec((block, PLANE), row),
            pl.BlockSpec((block, PLANE), row),
            pl.BlockSpec((block, 1), row),
            pl.BlockSpec((block, 1), row),
            pl.BlockSpec((block, 1), row),
            pl.BlockSpec((1, lanes), fixed),
            pl.BlockSpec((1, lanes), fixed),
            pl.BlockSpec((nm, block), lambda i: (0, i)),
        ],
        out_specs=[pl.BlockSpec((block, lanes), row), pl.BlockSpec((nm, lanes), fixed)],
        out_shape=[jax.ShapeDtypeStruct((nv, lanes), jnp.bfloat16), jax.ShapeDtypeStruct((nm, lanes), jnp.float32)],
        compiler_params=pltpu.CompilerParams(dimension_semantics=("arbitrary",)),
    )(adj, left, right, cx, cy, cz, coll, fluid, weigh)


def on_device(adjoint, collision, solid, codes):
    local_vel, width, plane = adjoint.shape
    start = lax.axis_index("vel") * local_vel
    speed_x, speed_y, speed_z, weigh, lift = tables(start, local_vel)
    count = lax.axis_size("space")
    ends = count - 1
    left = lax.ppermute(adjoint[:, width - 1], "space", [(i, i + 1) for i in range(ends)])
    right = lax.ppermute(adjoint[:, 0], "space", [(i + 1, i) for i in range(ends)])
    fluid = (1 - solid).astype(jnp.float32)
    starred_flat, partial_value = advance(
        adjoint.reshape(local_vel, width * plane),
        left,
        right,
        speed_x.reshape(local_vel, 1),
        speed_y.reshape(local_vel, 1),
        speed_z.reshape(local_vel, 1),
        collision.reshape(1, width * plane),
        fluid.reshape(1, width * plane),
        weigh,
    )
    moments = lax.psum(partial_value, "vel").reshape(NM, width, plane)
    cells_all = width * lax.axis_size("space") * plane
    squares = exchange_sum(jnp.sum(moments[0] * moments[0]), "space")
    scale = lax.rsqrt(squares / cells_all + 1e-06)
    inverse = fluid / (collision + wall_level(codes) + 6.0)
    source = collision[None] * moments
    fields = moments * fluid[None]
    for sweep in range(SWEEPS):
        fields = sweep_each(fields, source, inverse[None])
    delta = ((fields - moments) * scale).astype(jnp.bfloat16).reshape(NM, width * plane)
    added = jnp.dot(lift, delta, preferred_element_type=jnp.float32)
    corrected = (fluid.reshape(1, width * plane) * (starred_flat + added)).astype(jnp.bfloat16)
    return (corrected.reshape(local_vel, width, plane), fields * scale)


def solution(mesh):
    return jax.shard_map(
        on_device,
        mesh=mesh,
        in_specs=(P("vel", "space", None), P("space", None), P("space", None), P("space", None)),
        out_specs=(P("vel", "space", None), P(None, "space", None)),
        check_vma=False,
    )
```

```python
import math

import jax
import jax.numpy as jnp
from jax import lax
from jax.sharding import PartitionSpec as P
from jax.experimental import pallas as pl
from jax.experimental.pallas import tpu as pltpu

NV1 = 16
NM = 13
NY = 16
NZ = 16
SWEEPS = 3


TIME_STEP = 0.06
PLANE = NY * NZ


def with_halo(cells, sides, width):
    for axis, dim in sides:
        count = lax.axis_size(axis)
        ends = count - 1
        head = lax.slice_in_dim(cells, 0, width, axis=dim)
        tail = lax.slice_in_dim(cells, cells.shape[dim] - width, cells.shape[dim], axis=dim)
        cells = jnp.concatenate(
            [
                lax.ppermute(tail, axis, [(i, (i + 1) % count) for i in range(ends)]),
                cells,
                lax.ppermute(head, axis, [((i + 1) % count, i) for i in range(ends)]),
            ],
            axis=dim,
        )
    return cells


def exchange_sum(value, axis):
    count = lax.axis_size(axis)
    if count & (count - 1):
        return lax.psum(value, axis)
    stride = 1
    while stride < count:
        group = min(8 if (count // stride) % 8 == 0 and stride >= 16 else 4, count // stride)
        total = value
        for shift in range(1, group):
            pairs = []
            for i in range(count):
                member = (i // stride) % group
                target = i + (((member + shift) % group) - member) * stride
                pairs.append((i, target))
            total = total + lax.ppermute(value, axis, pairs)
        value = total
        stride *= group
    return value


def velocity_axes(start, count):
    index = start + jnp.arange(count, dtype=jnp.int32)
    spacing = 9.0 / NV1
    centre = (NV1 - 1) / 2.0
    along_x = ((index % NV1).astype(jnp.float32) - centre) * spacing
    along_z = ((index // NV1 % NV1).astype(jnp.float32) - centre) * spacing
    along_y = ((index // (NV1 * NV1)).astype(jnp.float32) - centre) * spacing
    return (along_x, along_y, along_z)


def tables(start, count):
    along_x, along_y, along_z = velocity_axes(start, count)
    speed = along_x * along_x + along_y * along_y + along_z * along_z
    unity = jnp.ones_like(along_x)
    basis = jnp.stack(
        [
            unity,
            along_x,
            along_y,
            along_z,
            (speed - 3.0) / math.sqrt(6.0),
            along_x * along_y,
            along_x * along_z,
            along_y * along_z,
            (along_x * along_x - along_y * along_y) / math.sqrt(2.0),
            (along_x * along_x + along_y * along_y - 2.0 * along_z * along_z) / math.sqrt(6.0),
            along_x * (speed - 5.0) / math.sqrt(10.0),
            along_y * (speed - 5.0) / math.sqrt(10.0),
            along_z * (speed - 5.0) / math.sqrt(10.0),
        ]
    )
    every_x, every_y, every_z = velocity_axes(0, NV1**3)
    total = jnp.sum(jnp.exp(-0.5 * (every_x * every_x + every_y * every_y + every_z * every_z)))
    weigh = (basis * jnp.exp(-0.5 * speed) / total).astype(jnp.bfloat16)
    lift = jnp.transpose(0.1 * basis * jnp.exp(-0.25 * speed)).astype(jnp.bfloat16)
    return (along_x, along_y, along_z, weigh, lift)


def wall_level(codes):
    return (
        0.5 * (codes == 1).astype(jnp.float32)
        + 1.5 * (codes == 2).astype(jnp.float32)
        + 4.0 * (codes == 3).astype(jnp.float32)
    )


def plane_around(fields):
    count, rows, plane = fields.shape
    cube = fields.reshape(count, rows, NY, NZ)
    padded = jnp.pad(cube, ((0, 0), (0, 0), (1, 1), (1, 1)))
    summed = (
        padded[:, :, 2:, 1:-1]
        + padded[:, :, :-2, 1:-1]
        + padded[:, :, 1:-1, 2:]
        + padded[:, :, 1:-1, :-2]
    )
    return summed.reshape(count, rows, plane)


def sweep_each(fields, source, inverse):
    widened = with_halo(fields.astype(jnp.bfloat16), (("space", 1),), 1).astype(fields.dtype)
    beside_all = widened[:, 2:] + widened[:, :-2] + plane_around(fields)
    return inverse * (source + beside_all)


def advance_kernel(adj_ref, left_ref, right_ref, cx_ref, cy_ref, cz_ref, coll_ref, fluid_ref, weigh_ref,
                   star_ref, part_ref):
    step = pl.program_id(0)
    g = adj_ref[...].astype(jnp.float32)
    rows, lanes = g.shape
    cx = cx_ref[...]
    cy = cy_ref[...]
    cz = cz_ref[...]
    left = left_ref[...].astype(jnp.float32)
    right = right_ref[...].astype(jnp.float32)
    after = jnp.concatenate([g[:, PLANE:], right], axis=1)
    before = jnp.concatenate([left, g[:, : lanes - PLANE]], axis=1)
    lane = lax.broadcasted_iota(jnp.int32, (1, lanes), 1)
    zpos = lane % NZ
    ypos = (lane // NZ) % (PLANE // NZ)
    y_next = jnp.where(ypos == PLANE // NZ - 1, 0.0, pltpu.roll(g, lanes - NZ, 1))
    y_prev = jnp.where(ypos == 0, 0.0, pltpu.roll(g, NZ, 1))
    z_next = jnp.where(zpos == NZ - 1, 0.0, pltpu.roll(g, lanes - 1, 1))
    z_prev = jnp.where(zpos == 0, 0.0, pltpu.roll(g, 1, 1))
    term_x = jnp.maximum(cx, 0.0) * (after - g) + jnp.minimum(cx, 0.0) * (g - before)
    term_y = jnp.maximum(cy, 0.0) * (y_next - g) + jnp.minimum(cy, 0.0) * (g - y_prev)
    term_z = jnp.maximum(cz, 0.0) * (z_next - g) + jnp.minimum(cz, 0.0) * (g - z_prev)
    advect = term_x + term_y + term_z
    starred = (fluid_ref[...] * (g + TIME_STEP * (advect - coll_ref[...] * g))).astype(jnp.bfloat16)
    star_ref[...] = starred
    partial = jnp.dot(weigh_ref[...], starred, preferred_element_type=jnp.float32)

    @pl.when(step == 0)
    def _():
        part_ref[...] = partial

    @pl.when(step > 0)
    def _():
        part_ref[...] += partial


def advance(adj, left, right, cx, cy, cz, coll, fluid, weigh, block=256):
    nv, lanes = adj.shape
    nm = weigh.shape[0]
    grid = (nv // block,)
    row = lambda i: (i, 0)
    fixed = lambda i: (0, 0)
    return pl.pallas_call(
        advance_kernel,
        grid=grid,
        in_specs=[
            pl.BlockSpec((block, lanes), row),
            pl.BlockSpec((block, PLANE), row),
            pl.BlockSpec((block, PLANE), row),
            pl.BlockSpec((block, 1), row),
            pl.BlockSpec((block, 1), row),
            pl.BlockSpec((block, 1), row),
            pl.BlockSpec((1, lanes), fixed),
            pl.BlockSpec((1, lanes), fixed),
            pl.BlockSpec((nm, block), lambda i: (0, i)),
        ],
        out_specs=[pl.BlockSpec((block, lanes), row), pl.BlockSpec((nm, lanes), fixed)],
        out_shape=[jax.ShapeDtypeStruct((nv, lanes), jnp.bfloat16), jax.ShapeDtypeStruct((nm, lanes), jnp.float32)],
        compiler_params=pltpu.CompilerParams(dimension_semantics=("arbitrary",)),
    )(adj, left, right, cx, cy, cz, coll, fluid, weigh)


def on_device(adjoint, collision, solid, codes):
    local_vel, width, plane = adjoint.shape
    start = lax.axis_index("vel") * local_vel
    speed_x, speed_y, speed_z, weigh, lift = tables(start, local_vel)
    count = lax.axis_size("space")
    ends = count - 1
    left = lax.ppermute(adjoint[:, width - 1], "space", [(i, i + 1) for i in range(ends)])
    right = lax.ppermute(adjoint[:, 0], "space", [(i + 1, i) for i in range(ends)])
    fluid = (1 - solid).astype(jnp.float32)
    starred_flat, partial_value = advance(
        adjoint.reshape(local_vel, width * plane),
        left,
        right,
        speed_x.reshape(local_vel, 1),
        speed_y.reshape(local_vel, 1),
        speed_z.reshape(local_vel, 1),
        collision.reshape(1, width * plane),
        fluid.reshape(1, width * plane),
        weigh,
    )
    moments = lax.psum(partial_value, "vel").reshape(NM, width, plane)
    cells_all = width * lax.axis_size("space") * plane
    squares = exchange_sum(jnp.sum(moments[0] * moments[0]), "space")
    scale = lax.rsqrt(squares / cells_all + 1e-06)
    inverse = fluid / (collision + wall_level(codes) + 6.0)
    source = collision[None] * moments
    fields = moments * fluid[None]
    for sweep in range(SWEEPS):
        fields = sweep_each(fields, source, inverse[None])
    delta = ((fields - moments) * scale).astype(jnp.bfloat16).reshape(NM, width * plane)
    added = jnp.dot(lift, delta, preferred_element_type=jnp.float32)
    corrected = (fluid.reshape(1, width * plane) * (starred_flat + added)).astype(jnp.bfloat16)
    return (corrected.reshape(local_vel, width, plane), fields * scale)


def solution(mesh):
    return jax.shard_map(
        on_device,
        mesh=mesh,
        in_specs=(P("vel", "space", None), P("space", None), P("space", None), P("space", None)),
        out_specs=(P("vel", "space", None), P(None, "space", None)),
        check_vma=False,
    )
```

```python
import math

import jax
import jax.numpy as jnp
from jax import lax
from jax.sharding import PartitionSpec as P
from jax.experimental import pallas as pl
from jax.experimental.pallas import tpu as pltpu

NV1 = 16
NM = 13
NY = 16
NZ = 16
SWEEPS = 3


TIME_STEP = 0.06
PLANE = NY * NZ


def with_halo(cells, sides, width):
    for axis, dim in sides:
        count = lax.axis_size(axis)
        ends = count - 1
        head = lax.slice_in_dim(cells, 0, width, axis=dim)
        tail = lax.slice_in_dim(cells, cells.shape[dim] - width, cells.shape[dim], axis=dim)
        cells = jnp.concatenate(
            [
                lax.ppermute(tail, axis, [(i, (i + 1) % count) for i in range(ends)]),
                cells,
                lax.ppermute(head, axis, [((i + 1) % count, i) for i in range(ends)]),
            ],
            axis=dim,
        )
    return cells


def exchange_sum(value, axis):
    count = lax.axis_size(axis)
    if count & (count - 1):
        return lax.psum(value, axis)
    step = 1
    while step < count:
        value = value + lax.ppermute(value, axis, [(i, i ^ step) for i in range(count)])
        step *= 2
    return value


def velocity_axes(start, count):
    index = start + jnp.arange(count, dtype=jnp.int32)
    spacing = 9.0 / NV1
    centre = (NV1 - 1) / 2.0
    along_x = ((index % NV1).astype(jnp.float32) - centre) * spacing
    along_z = ((index // NV1 % NV1).astype(jnp.float32) - centre) * spacing
    along_y = ((index // (NV1 * NV1)).astype(jnp.float32) - centre) * spacing
    return (along_x, along_y, along_z)


def tables(start, count):
    along_x, along_y, along_z = velocity_axes(start, count)
    speed = along_x * along_x + along_y * along_y + along_z * along_z
    unity = jnp.ones_like(along_x)
    basis = jnp.stack(
        [
            unity,
            along_x,
            along_y,
            along_z,
            (speed - 3.0) / math.sqrt(6.0),
            along_x * along_y,
            along_x * along_z,
            along_y * along_z,
            (along_x * along_x - along_y * along_y) / math.sqrt(2.0),
            (along_x * along_x + along_y * along_y - 2.0 * along_z * along_z) / math.sqrt(6.0),
            along_x * (speed - 5.0) / math.sqrt(10.0),
            along_y * (speed - 5.0) / math.sqrt(10.0),
            along_z * (speed - 5.0) / math.sqrt(10.0),
        ]
    )
    every_x, every_y, every_z = velocity_axes(0, NV1**3)
    total = jnp.sum(jnp.exp(-0.5 * (every_x * every_x + every_y * every_y + every_z * every_z)))
    weigh = (basis * jnp.exp(-0.5 * speed) / total).astype(jnp.bfloat16)
    lift = jnp.transpose(0.1 * basis * jnp.exp(-0.25 * speed)).astype(jnp.bfloat16)
    return (along_x, along_y, along_z, weigh, lift)


def wall_level(codes):
    return (
        0.5 * (codes == 1).astype(jnp.float32)
        + 1.5 * (codes == 2).astype(jnp.float32)
        + 4.0 * (codes == 3).astype(jnp.float32)
    )


def plane_around(fields):
    count, rows, plane = fields.shape
    cube = fields.reshape(count, rows, NY, NZ)
    padded = jnp.pad(cube, ((0, 0), (0, 0), (1, 1), (1, 1)))
    summed = (
        padded[:, :, 2:, 1:-1]
        + padded[:, :, :-2, 1:-1]
        + padded[:, :, 1:-1, 2:]
        + padded[:, :, 1:-1, :-2]
    )
    return summed.reshape(count, rows, plane)


def sweep_each(fields, source, inverse):
    widened = with_halo(fields.astype(jnp.bfloat16), (("space", 1),), 1).astype(fields.dtype)
    beside_all = widened[:, 2:] + widened[:, :-2] + plane_around(fields)
    return inverse * (source + beside_all)


def advance_kernel(adj_ref, left_ref, right_ref, cx_ref, cy_ref, cz_ref, coll_ref, fluid_ref, weigh_ref,
                   star_ref, part_ref):
    step = pl.program_id(0)
    g = adj_ref[...].astype(jnp.float32)
    rows, lanes = g.shape
    cx = cx_ref[...]
    cy = cy_ref[...]
    cz = cz_ref[...]
    half = NV1 // 2
    blank = jnp.zeros((rows // NV1, half, PLANE), jnp.float32)
    left = left_ref[...].astype(jnp.float32).reshape(rows // NV1, half, PLANE)
    right = right_ref[...].astype(jnp.float32).reshape(rows // NV1, half, PLANE)
    left = jnp.concatenate([left, blank], axis=1).reshape(rows, PLANE)
    right = jnp.concatenate([blank, right], axis=1).reshape(rows, PLANE)
    after = jnp.concatenate([g[:, PLANE:], right], axis=1)
    before = jnp.concatenate([left, g[:, : lanes - PLANE]], axis=1)
    lane = lax.broadcasted_iota(jnp.int32, (1, lanes), 1)
    zpos = lane % NZ
    ypos = (lane // NZ) % (PLANE // NZ)
    y_next = jnp.where(ypos == PLANE // NZ - 1, 0.0, pltpu.roll(g, lanes - NZ, 1))
    y_prev = jnp.where(ypos == 0, 0.0, pltpu.roll(g, NZ, 1))
    z_next = jnp.where(zpos == NZ - 1, 0.0, pltpu.roll(g, lanes - 1, 1))
    z_prev = jnp.where(zpos == 0, 0.0, pltpu.roll(g, 1, 1))
    term_x = jnp.maximum(cx, 0.0) * (after - g) + jnp.minimum(cx, 0.0) * (g - before)
    term_y = jnp.maximum(cy, 0.0) * (y_next - g) + jnp.minimum(cy, 0.0) * (g - y_prev)
    term_z = jnp.maximum(cz, 0.0) * (z_next - g) + jnp.minimum(cz, 0.0) * (g - z_prev)
    advect = term_x + term_y + term_z
    starred = (fluid_ref[...] * (g + TIME_STEP * (advect - coll_ref[...] * g))).astype(jnp.bfloat16)
    star_ref[...] = starred
    partial = jnp.dot(weigh_ref[...], starred, preferred_element_type=jnp.float32)

    @pl.when(step == 0)
    def _():
        part_ref[...] = partial

    @pl.when(step > 0)
    def _():
        part_ref[...] += partial


def advance(adj, left, right, cx, cy, cz, coll, fluid, weigh, block=256):
    nv, lanes = adj.shape
    nm = weigh.shape[0]
    grid = (nv // block,)
    row = lambda i: (i, 0)
    fixed = lambda i: (0, 0)
    return pl.pallas_call(
        advance_kernel,
        grid=grid,
        in_specs=[
            pl.BlockSpec((block, lanes), row),
            pl.BlockSpec((block // 2, PLANE), row),
            pl.BlockSpec((block // 2, PLANE), row),
            pl.BlockSpec((block, 1), row),
            pl.BlockSpec((block, 1), row),
            pl.BlockSpec((block, 1), row),
            pl.BlockSpec((1, lanes), fixed),
            pl.BlockSpec((1, lanes), fixed),
            pl.BlockSpec((nm, block), lambda i: (0, i)),
        ],
        out_specs=[pl.BlockSpec((block, lanes), row), pl.BlockSpec((nm, lanes), fixed)],
        out_shape=[jax.ShapeDtypeStruct((nv, lanes), jnp.bfloat16), jax.ShapeDtypeStruct((nm, lanes), jnp.float32)],
        compiler_params=pltpu.CompilerParams(dimension_semantics=("arbitrary",)),
    )(adj, left, right, cx, cy, cz, coll, fluid, weigh)


def on_device(adjoint, collision, solid, codes):
    local_vel, width, plane = adjoint.shape
    start = lax.axis_index("vel") * local_vel
    speed_x, speed_y, speed_z, weigh, lift = tables(start, local_vel)
    count = lax.axis_size("space")
    ends = count - 1
    flat = adjoint.reshape(local_vel, width * plane)
    grouped = flat.reshape(local_vel // NV1, NV1, width * plane)
    half = NV1 // 2
    tail = grouped[:, :half, (width - 1) * plane :].reshape(local_vel // 2, plane)
    head = grouped[:, half:, :plane].reshape(local_vel // 2, plane)
    left = lax.ppermute(tail, "space", [(i, i + 1) for i in range(ends)])
    right = lax.ppermute(head, "space", [(i + 1, i) for i in range(ends)])
    fluid = (1 - solid).astype(jnp.float32)
    starred_flat, partial_value = advance(
        flat,
        left,
        right,
        speed_x.reshape(local_vel, 1),
        speed_y.reshape(local_vel, 1),
        speed_z.reshape(local_vel, 1),
        collision.reshape(1, width * plane),
        fluid.reshape(1, width * plane),
        weigh,
    )
    moments = lax.psum(partial_value, "vel").reshape(NM, width, plane)
    cells_all = width * lax.axis_size("space") * plane
    squares = exchange_sum(jnp.sum(moments[0] * moments[0]), "space")
    scale = lax.rsqrt(squares / cells_all + 1e-06)
    inverse = fluid / (collision + wall_level(codes) + 6.0)
    source = collision[None] * moments
    fields = moments * fluid[None]
    for sweep in range(SWEEPS):
        fields = sweep_each(fields, source, inverse[None])
    delta = ((fields - moments) * scale).astype(jnp.bfloat16).reshape(NM, width * plane)
    added = jnp.dot(lift, delta, preferred_element_type=jnp.float32)
    corrected = (fluid.reshape(1, width * plane) * (starred_flat + added)).astype(jnp.bfloat16)
    return (corrected.reshape(local_vel, width, plane), fields * scale)


def solution(mesh):
    return jax.shard_map(
        on_device,
        mesh=mesh,
        in_specs=(P("vel", "space", None), P("space", None), P("space", None), P("space", None)),
        out_specs=(P("vel", "space", None), P(None, "space", None)),
        check_vma=False,
    )
```

```python
import math

import jax
import jax.numpy as jnp
from jax import lax
from jax.sharding import PartitionSpec as P
from jax.experimental import pallas as pl
from jax.experimental.pallas import tpu as pltpu

NV1 = 16
NM = 13
NY = 16
NZ = 16
SWEEPS = 3


TIME_STEP = 0.06
PLANE = NY * NZ


def with_halo(cells, sides, width):
    for axis, dim in sides:
        count = lax.axis_size(axis)
        ends = count - 1
        head = lax.slice_in_dim(cells, 0, width, axis=dim)
        tail = lax.slice_in_dim(cells, cells.shape[dim] - width, cells.shape[dim], axis=dim)
        cells = jnp.concatenate(
            [
                lax.ppermute(tail, axis, [(i, (i + 1) % count) for i in range(ends)]),
                cells,
                lax.ppermute(head, axis, [((i + 1) % count, i) for i in range(ends)]),
            ],
            axis=dim,
        )
    return cells


def exchange_sum(value, axis):
    count = lax.axis_size(axis)
    if count & (count - 1):
        return lax.psum(value, axis)
    step = 1
    while step < count:
        value = value + lax.ppermute(value, axis, [(i, i ^ step) for i in range(count)])
        step *= 2
    return value


def velocity_axes(start, count):
    index = start + jnp.arange(count, dtype=jnp.int32)
    spacing = 9.0 / NV1
    centre = (NV1 - 1) / 2.0
    along_x = ((index % NV1).astype(jnp.float32) - centre) * spacing
    along_z = ((index // NV1 % NV1).astype(jnp.float32) - centre) * spacing
    along_y = ((index // (NV1 * NV1)).astype(jnp.float32) - centre) * spacing
    return (along_x, along_y, along_z)


def tables(start, count):
    along_x, along_y, along_z = velocity_axes(start, count)
    speed = along_x * along_x + along_y * along_y + along_z * along_z
    unity = jnp.ones_like(along_x)
    basis = jnp.stack(
        [
            unity,
            along_x,
            along_y,
            along_z,
            (speed - 3.0) / math.sqrt(6.0),
            along_x * along_y,
            along_x * along_z,
            along_y * along_z,
            (along_x * along_x - along_y * along_y) / math.sqrt(2.0),
            (along_x * along_x + along_y * along_y - 2.0 * along_z * along_z) / math.sqrt(6.0),
            along_x * (speed - 5.0) / math.sqrt(10.0),
            along_y * (speed - 5.0) / math.sqrt(10.0),
            along_z * (speed - 5.0) / math.sqrt(10.0),
        ]
    )
    every_x, every_y, every_z = velocity_axes(0, NV1**3)
    total = jnp.sum(jnp.exp(-0.5 * (every_x * every_x + every_y * every_y + every_z * every_z)))
    weigh = (basis * jnp.exp(-0.5 * speed) / total).astype(jnp.bfloat16)
    lift = jnp.transpose(0.1 * basis * jnp.exp(-0.25 * speed)).astype(jnp.bfloat16)
    return (along_x, along_y, along_z, weigh, lift)


def wall_level(codes):
    return (
        0.5 * (codes == 1).astype(jnp.float32)
        + 1.5 * (codes == 2).astype(jnp.float32)
        + 4.0 * (codes == 3).astype(jnp.float32)
    )


def plane_around(fields):
    count, rows, plane = fields.shape
    cube = fields.reshape(count, rows, NY, NZ)
    padded = jnp.pad(cube, ((0, 0), (0, 0), (1, 1), (1, 1)))
    summed = (
        padded[:, :, 2:, 1:-1]
        + padded[:, :, :-2, 1:-1]
        + padded[:, :, 1:-1, 2:]
        + padded[:, :, 1:-1, :-2]
    )
    return summed.reshape(count, rows, plane)


def sweep_all(moments, fluid, collision, kappa):
    count = lax.axis_size("space")
    ends = count - 1
    width = moments.shape[1]
    depth = SWEEPS
    pack = jnp.concatenate([moments, jnp.stack([fluid, collision, kappa])], axis=0)
    before = lax.ppermute(pack[:, width - depth :], "space", [(i, i + 1) for i in range(ends)])
    after = lax.ppermute(pack[:, :depth], "space", [(i + 1, i) for i in range(ends)])
    wide = jnp.concatenate([before, pack, after], axis=1)
    total = wide.shape[1]
    grown = wide[:NM]
    inverse = wide[NM] / (wide[NM + 1] + wide[NM + 2] + 6.0)
    source = wide[NM + 1][None] * grown
    fields = grown * wide[NM][None]
    for sweep in range(SWEEPS):
        lo, hi = sweep + 1, total - 1 - sweep
        beside_all = fields[:, 2:] + fields[:, :-2] + plane_around(fields[:, 1:-1])
        fields = inverse[None, lo:hi] * (source[:, lo:hi] + beside_all)
    return fields


def advance_kernel(adj_ref, left_ref, right_ref, cx_ref, cy_ref, cz_ref, coll_ref, fluid_ref, weigh_ref,
                   star_ref, part_ref):
    step = pl.program_id(0)
    g = adj_ref[...].astype(jnp.float32)
    rows, lanes = g.shape
    cx = cx_ref[...]
    cy = cy_ref[...]
    cz = cz_ref[...]
    half = NV1 // 2
    blank = jnp.zeros((rows // NV1, half, PLANE), jnp.float32)
    left = left_ref[...].astype(jnp.float32).reshape(rows // NV1, half, PLANE)
    right = right_ref[...].astype(jnp.float32).reshape(rows // NV1, half, PLANE)
    left = jnp.concatenate([left, blank], axis=1).reshape(rows, PLANE)
    right = jnp.concatenate([blank, right], axis=1).reshape(rows, PLANE)
    after = jnp.concatenate([g[:, PLANE:], right], axis=1)
    before = jnp.concatenate([left, g[:, : lanes - PLANE]], axis=1)
    lane = lax.broadcasted_iota(jnp.int32, (1, lanes), 1)
    zpos = lane % NZ
    ypos = (lane // NZ) % (PLANE // NZ)
    y_next = jnp.where(ypos == PLANE // NZ - 1, 0.0, pltpu.roll(g, lanes - NZ, 1))
    y_prev = jnp.where(ypos == 0, 0.0, pltpu.roll(g, NZ, 1))
    z_next = jnp.where(zpos == NZ - 1, 0.0, pltpu.roll(g, lanes - 1, 1))
    z_prev = jnp.where(zpos == 0, 0.0, pltpu.roll(g, 1, 1))
    term_x = jnp.maximum(cx, 0.0) * (after - g) + jnp.minimum(cx, 0.0) * (g - before)
    term_y = jnp.maximum(cy, 0.0) * (y_next - g) + jnp.minimum(cy, 0.0) * (g - y_prev)
    term_z = jnp.maximum(cz, 0.0) * (z_next - g) + jnp.minimum(cz, 0.0) * (g - z_prev)
    advect = term_x + term_y + term_z
    starred = (fluid_ref[...] * (g + TIME_STEP * (advect - coll_ref[...] * g))).astype(jnp.bfloat16)
    star_ref[...] = starred
    partial = jnp.dot(weigh_ref[...], starred, preferred_element_type=jnp.float32)

    @pl.when(step == 0)
    def _():
        part_ref[...] = partial

    @pl.when(step > 0)
    def _():
        part_ref[...] += partial


def advance(adj, left, right, cx, cy, cz, coll, fluid, weigh, block=256):
    nv, lanes = adj.shape
    nm = weigh.shape[0]
    grid = (nv // block,)
    row = lambda i: (i, 0)
    fixed = lambda i: (0, 0)
    return pl.pallas_call(
        advance_kernel,
        grid=grid,
        in_specs=[
            pl.BlockSpec((block, lanes), row),
            pl.BlockSpec((block // 2, PLANE), row),
            pl.BlockSpec((block // 2, PLANE), row),
            pl.BlockSpec((block, 1), row),
            pl.BlockSpec((block, 1), row),
            pl.BlockSpec((block, 1), row),
            pl.BlockSpec((1, lanes), fixed),
            pl.BlockSpec((1, lanes), fixed),
            pl.BlockSpec((nm, block), lambda i: (0, i)),
        ],
        out_specs=[pl.BlockSpec((block, lanes), row), pl.BlockSpec((nm, lanes), fixed)],
        out_shape=[jax.ShapeDtypeStruct((nv, lanes), jnp.bfloat16), jax.ShapeDtypeStruct((nm, lanes), jnp.float32)],
        compiler_params=pltpu.CompilerParams(dimension_semantics=("arbitrary",)),
    )(adj, left, right, cx, cy, cz, coll, fluid, weigh)


def on_device(adjoint, collision, solid, codes):
    local_vel, width, plane = adjoint.shape
    start = lax.axis_index("vel") * local_vel
    speed_x, speed_y, speed_z, weigh, lift = tables(start, local_vel)
    count = lax.axis_size("space")
    ends = count - 1
    flat = lax.optimization_barrier(adjoint.reshape(local_vel, width * plane))
    grouped = flat.reshape(local_vel // NV1, NV1, width * plane)
    half = NV1 // 2
    tail = grouped[:, :half, (width - 1) * plane :].reshape(local_vel // 2, plane)
    head = grouped[:, half:, :plane].reshape(local_vel // 2, plane)
    left = lax.ppermute(tail, "space", [(i, i + 1) for i in range(ends)])
    right = lax.ppermute(head, "space", [(i + 1, i) for i in range(ends)])
    fluid = (1 - solid).astype(jnp.float32)
    starred_flat, partial_value = advance(
        flat,
        left,
        right,
        speed_x.reshape(local_vel, 1),
        speed_y.reshape(local_vel, 1),
        speed_z.reshape(local_vel, 1),
        collision.reshape(1, width * plane),
        fluid.reshape(1, width * plane),
        weigh,
    )
    moments = lax.psum(partial_value, "vel").reshape(NM, width, plane)
    cells_all = width * lax.axis_size("space") * plane
    squares = exchange_sum(jnp.sum(moments[0] * moments[0]), "space")
    scale = lax.rsqrt(squares / cells_all + 1e-06)
    fields = sweep_all(moments, fluid, collision, wall_level(codes))
    delta = ((fields - moments) * scale).astype(jnp.bfloat16).reshape(NM, width * plane)
    added = jnp.dot(lift, delta, preferred_element_type=jnp.float32)
    corrected = (fluid.reshape(1, width * plane) * (starred_flat + added)).astype(jnp.bfloat16)
    return (corrected.reshape(local_vel, width, plane), fields * scale)


def solution(mesh):
    return jax.shard_map(
        on_device,
        mesh=mesh,
        in_specs=(P("vel", "space", None), P("space", None), P("space", None), P("space", None)),
        out_specs=(P("vel", "space", None), P(None, "space", None)),
        check_vma=False,
    )
```

```python
import math

import jax
import jax.numpy as jnp
from jax import lax
from jax.sharding import PartitionSpec as P
from jax.experimental import pallas as pl
from jax.experimental.pallas import tpu as pltpu

NV1 = 16
NM = 13
NY = 16
NZ = 16
SWEEPS = 3


TIME_STEP = 0.06
PLANE = NY * NZ


def with_halo(cells, sides, width):
    for axis, dim in sides:
        count = lax.axis_size(axis)
        ends = count - 1
        head = lax.slice_in_dim(cells, 0, width, axis=dim)
        tail = lax.slice_in_dim(cells, cells.shape[dim] - width, cells.shape[dim], axis=dim)
        cells = jnp.concatenate(
            [
                lax.ppermute(tail, axis, [(i, (i + 1) % count) for i in range(ends)]),
                cells,
                lax.ppermute(head, axis, [((i + 1) % count, i) for i in range(ends)]),
            ],
            axis=dim,
        )
    return cells


def exchange_sum(value, axis):
    count = lax.axis_size(axis)
    if count & (count - 1):
        return lax.psum(value, axis)
    step = 1
    while step < count:
        value = value + lax.ppermute(value, axis, [(i, i ^ step) for i in range(count)])
        step *= 2
    return value


def velocity_axes(start, count):
    index = start + jnp.arange(count, dtype=jnp.int32)
    spacing = 9.0 / NV1
    centre = (NV1 - 1) / 2.0
    along_x = ((index % NV1).astype(jnp.float32) - centre) * spacing
    along_z = ((index // NV1 % NV1).astype(jnp.float32) - centre) * spacing
    along_y = ((index // (NV1 * NV1)).astype(jnp.float32) - centre) * spacing
    return (along_x, along_y, along_z)


def tables(start, count):
    along_x, along_y, along_z = velocity_axes(start, count)
    speed = along_x * along_x + along_y * along_y + along_z * along_z
    unity = jnp.ones_like(along_x)
    basis = jnp.stack(
        [
            unity,
            along_x,
            along_y,
            along_z,
            (speed - 3.0) / math.sqrt(6.0),
            along_x * along_y,
            along_x * along_z,
            along_y * along_z,
            (along_x * along_x - along_y * along_y) / math.sqrt(2.0),
            (along_x * along_x + along_y * along_y - 2.0 * along_z * along_z) / math.sqrt(6.0),
            along_x * (speed - 5.0) / math.sqrt(10.0),
            along_y * (speed - 5.0) / math.sqrt(10.0),
            along_z * (speed - 5.0) / math.sqrt(10.0),
        ]
    )
    every_x, every_y, every_z = velocity_axes(0, NV1**3)
    total = jnp.sum(jnp.exp(-0.5 * (every_x * every_x + every_y * every_y + every_z * every_z)))
    weigh = (basis * jnp.exp(-0.5 * speed) / total).astype(jnp.bfloat16)
    lift = jnp.transpose(0.1 * basis * jnp.exp(-0.25 * speed)).astype(jnp.bfloat16)
    return (along_x, along_y, along_z, weigh, lift)


def wall_level(codes):
    return (
        0.5 * (codes == 1).astype(jnp.float32)
        + 1.5 * (codes == 2).astype(jnp.float32)
        + 4.0 * (codes == 3).astype(jnp.float32)
    )


def plane_around(fields):
    count, rows, plane = fields.shape
    cube = fields.reshape(count, rows, NY, NZ)
    padded = jnp.pad(cube, ((0, 0), (0, 0), (1, 1), (1, 1)))
    summed = (
        padded[:, :, 2:, 1:-1]
        + padded[:, :, :-2, 1:-1]
        + padded[:, :, 1:-1, 2:]
        + padded[:, :, 1:-1, :-2]
    )
    return summed.reshape(count, rows, plane)


def sweep_all(moments, fluid, collision, kappa):
    count = lax.axis_size("space")
    ends = count - 1
    width = moments.shape[1]
    depth = SWEEPS
    pack = jnp.concatenate([moments, jnp.stack([fluid, collision, kappa])], axis=0)
    before = lax.ppermute(pack[:, width - depth :], "space", [(i, i + 1) for i in range(ends)])
    after = lax.ppermute(pack[:, :depth], "space", [(i + 1, i) for i in range(ends)])
    wide = jnp.concatenate([before, pack, after], axis=1)
    total = wide.shape[1]
    grown = wide[:NM]
    inverse = wide[NM] / (wide[NM + 1] + wide[NM + 2] + 6.0)
    source = wide[NM + 1][None] * grown
    fields = grown * wide[NM][None]
    for sweep in range(SWEEPS):
        lo, hi = sweep + 1, total - 1 - sweep
        beside_all = fields[:, 2:] + fields[:, :-2] + plane_around(fields[:, 1:-1])
        fields = inverse[None, lo:hi] * (source[:, lo:hi] + beside_all)
    return fields


def advance_kernel(adj_ref, left_ref, right_ref, cx_ref, cy_ref, cz_ref, coll_ref, fluid_ref, weigh_ref,
                   star_ref, part_ref):
    step = pl.program_id(0)
    g = adj_ref[...].astype(jnp.float32)
    rows, lanes = g.shape
    cx = cx_ref[...]
    cy = cy_ref[...]
    cz = cz_ref[...]
    half = NV1 // 2
    blank = jnp.zeros((rows // NV1, half, PLANE), jnp.float32)
    left = left_ref[...].astype(jnp.float32).reshape(rows // NV1, half, PLANE)
    right = right_ref[...].astype(jnp.float32).reshape(rows // NV1, half, PLANE)
    left = jnp.concatenate([left, blank], axis=1).reshape(rows, PLANE)
    right = jnp.concatenate([blank, right], axis=1).reshape(rows, PLANE)
    after = jnp.concatenate([g[:, PLANE:], right], axis=1)
    before = jnp.concatenate([left, g[:, : lanes - PLANE]], axis=1)
    lane = lax.broadcasted_iota(jnp.int32, (1, lanes), 1)
    zpos = lane % NZ
    ypos = (lane // NZ) % (PLANE // NZ)
    y_next = jnp.where(ypos == PLANE // NZ - 1, 0.0, pltpu.roll(g, lanes - NZ, 1))
    y_prev = jnp.where(ypos == 0, 0.0, pltpu.roll(g, NZ, 1))
    z_next = jnp.where(zpos == NZ - 1, 0.0, pltpu.roll(g, lanes - 1, 1))
    z_prev = jnp.where(zpos == 0, 0.0, pltpu.roll(g, 1, 1))
    term_x = jnp.maximum(cx, 0.0) * (after - g) + jnp.minimum(cx, 0.0) * (g - before)
    term_y = jnp.maximum(cy, 0.0) * (y_next - g) + jnp.minimum(cy, 0.0) * (g - y_prev)
    term_z = jnp.maximum(cz, 0.0) * (z_next - g) + jnp.minimum(cz, 0.0) * (g - z_prev)
    advect = term_x + term_y + term_z
    starred = (fluid_ref[...] * (g + TIME_STEP * (advect - coll_ref[...] * g))).astype(jnp.bfloat16)
    star_ref[...] = starred
    partial = jnp.dot(weigh_ref[...], starred, preferred_element_type=jnp.float32)

    @pl.when(step == 0)
    def _():
        part_ref[...] = partial

    @pl.when(step > 0)
    def _():
        part_ref[...] += partial


def advance(adj, left, right, cx, cy, cz, coll, fluid, weigh, block=256):
    nv, lanes = adj.shape
    nm = weigh.shape[0]
    grid = (nv // block,)
    row = lambda i: (i, 0)
    fixed = lambda i: (0, 0)
    return pl.pallas_call(
        advance_kernel,
        grid=grid,
        in_specs=[
            pl.BlockSpec((block, lanes), row),
            pl.BlockSpec((block // 2, PLANE), row),
            pl.BlockSpec((block // 2, PLANE), row),
            pl.BlockSpec((block, 1), row),
            pl.BlockSpec((block, 1), row),
            pl.BlockSpec((block, 1), row),
            pl.BlockSpec((1, lanes), fixed),
            pl.BlockSpec((1, lanes), fixed),
            pl.BlockSpec((nm, block), lambda i: (0, i)),
        ],
        out_specs=[pl.BlockSpec((block, lanes), row), pl.BlockSpec((nm, lanes), fixed)],
        out_shape=[jax.ShapeDtypeStruct((nv, lanes), jnp.bfloat16), jax.ShapeDtypeStruct((nm, lanes), jnp.float32)],
        compiler_params=pltpu.CompilerParams(dimension_semantics=("arbitrary",)),
    )(adj, left, right, cx, cy, cz, coll, fluid, weigh)


def on_device(adjoint, collision, solid, codes):
    local_vel, width, plane = adjoint.shape
    start = lax.axis_index("vel") * local_vel
    speed_x, speed_y, speed_z, weigh, lift = tables(start, local_vel)
    count = lax.axis_size("space")
    ends = count - 1
    flat = lax.optimization_barrier(adjoint.reshape(local_vel, width * plane))
    grouped = flat.reshape(local_vel // NV1, NV1, width * plane)
    half = NV1 // 2
    tail = grouped[:, :half, (width - 1) * plane :].reshape(local_vel // 2, plane)
    head = grouped[:, half:, :plane].reshape(local_vel // 2, plane)
    left = lax.ppermute(tail, "space", [(i, i + 1) for i in range(ends)])
    right = lax.ppermute(head, "space", [(i + 1, i) for i in range(ends)])
    fluid = (1 - solid).astype(jnp.float32)
    starred_flat, partial_value = advance(
        flat,
        left,
        right,
        speed_x.reshape(local_vel, 1),
        speed_y.reshape(local_vel, 1),
        speed_z.reshape(local_vel, 1),
        collision.reshape(1, width * plane),
        fluid.reshape(1, width * plane),
        weigh,
    )
    moments = lax.psum(partial_value, "vel").reshape(NM, width, plane)
    cells_all = width * lax.axis_size("space") * plane
    own = jnp.where(lax.axis_index("vel") == 0, jnp.sum(moments[0] * moments[0]), 0.0)
    squares = lax.psum(jnp.zeros((16384,), jnp.float32).at[0].set(own), ("space", "vel"))[0]
    scale = lax.rsqrt(squares / cells_all + 1e-06)
    fields = sweep_all(moments, fluid, collision, wall_level(codes))
    delta = ((fields - moments) * scale).astype(jnp.bfloat16).reshape(NM, width * plane)
    added = jnp.dot(lift, delta, preferred_element_type=jnp.float32)
    corrected = (fluid.reshape(1, width * plane) * (starred_flat + added)).astype(jnp.bfloat16)
    return (corrected.reshape(local_vel, width, plane), fields * scale)


def solution(mesh):
    return jax.shard_map(
        on_device,
        mesh=mesh,
        in_specs=(P("vel", "space", None), P("space", None), P("space", None), P("space", None)),
        out_specs=(P("vel", "space", None), P(None, "space", None)),
        check_vma=False,
    )
```

```python
import math

import jax
import jax.numpy as jnp
from jax import lax
from jax.sharding import PartitionSpec as P
from jax.experimental import pallas as pl
from jax.experimental.pallas import tpu as pltpu

NV1 = 16
NM = 13
NY = 16
NZ = 16
SWEEPS = 3


TIME_STEP = 0.06
PLANE = NY * NZ


def with_halo(cells, sides, width):
    for axis, dim in sides:
        count = lax.axis_size(axis)
        ends = count - 1
        head = lax.slice_in_dim(cells, 0, width, axis=dim)
        tail = lax.slice_in_dim(cells, cells.shape[dim] - width, cells.shape[dim], axis=dim)
        cells = jnp.concatenate(
            [
                lax.ppermute(tail, axis, [(i, (i + 1) % count) for i in range(ends)]),
                cells,
                lax.ppermute(head, axis, [((i + 1) % count, i) for i in range(ends)]),
            ],
            axis=dim,
        )
    return cells


def exchange_sum(value, axis):
    count = lax.axis_size(axis)
    if count & (count - 1):
        return lax.psum(value, axis)
    step = 1
    while step < count:
        value = value + lax.ppermute(value, axis, [(i, i ^ step) for i in range(count)])
        step *= 2
    return value


def velocity_axes(start, count):
    index = start + jnp.arange(count, dtype=jnp.int32)
    spacing = 9.0 / NV1
    centre = (NV1 - 1) / 2.0
    along_x = ((index % NV1).astype(jnp.float32) - centre) * spacing
    along_z = ((index // NV1 % NV1).astype(jnp.float32) - centre) * spacing
    along_y = ((index // (NV1 * NV1)).astype(jnp.float32) - centre) * spacing
    return (along_x, along_y, along_z)


def tables(start, count):
    along_x, along_y, along_z = velocity_axes(start, count)
    speed = along_x * along_x + along_y * along_y + along_z * along_z
    unity = jnp.ones_like(along_x)
    basis = jnp.stack(
        [
            unity,
            along_x,
            along_y,
            along_z,
            (speed - 3.0) / math.sqrt(6.0),
            along_x * along_y,
            along_x * along_z,
            along_y * along_z,
            (along_x * along_x - along_y * along_y) / math.sqrt(2.0),
            (along_x * along_x + along_y * along_y - 2.0 * along_z * along_z) / math.sqrt(6.0),
            along_x * (speed - 5.0) / math.sqrt(10.0),
            along_y * (speed - 5.0) / math.sqrt(10.0),
            along_z * (speed - 5.0) / math.sqrt(10.0),
        ]
    )
    every_x, every_y, every_z = velocity_axes(0, NV1**3)
    total = jnp.sum(jnp.exp(-0.5 * (every_x * every_x + every_y * every_y + every_z * every_z)))
    weigh = (basis * jnp.exp(-0.5 * speed) / total).astype(jnp.bfloat16)
    lift = jnp.transpose(0.1 * basis * jnp.exp(-0.25 * speed)).astype(jnp.bfloat16)
    return (along_x, along_y, along_z, weigh, lift)


def wall_level(codes):
    return (
        0.5 * (codes == 1).astype(jnp.float32)
        + 1.5 * (codes == 2).astype(jnp.float32)
        + 4.0 * (codes == 3).astype(jnp.float32)
    )


def plane_around(fields):
    count, rows, plane = fields.shape
    cube = fields.reshape(count, rows, NY, NZ)
    padded = jnp.pad(cube, ((0, 0), (0, 0), (1, 1), (1, 1)))
    summed = (
        padded[:, :, 2:, 1:-1]
        + padded[:, :, :-2, 1:-1]
        + padded[:, :, 1:-1, 2:]
        + padded[:, :, 1:-1, :-2]
    )
    return summed.reshape(count, rows, plane)


def sweep_all(moments, fluid, collision, kappa):
    count = lax.axis_size("space")
    ends = count - 1
    width = moments.shape[1]
    depth = SWEEPS
    pack = jnp.concatenate([moments, jnp.stack([fluid, collision, kappa])], axis=0)
    before = lax.ppermute(pack[:, width - depth :], "space", [(i, i + 1) for i in range(ends)])
    after = lax.ppermute(pack[:, :depth], "space", [(i + 1, i) for i in range(ends)])
    wide = jnp.concatenate([before, pack, after], axis=1)
    total = wide.shape[1]
    grown = wide[:NM]
    inverse = wide[NM] / (wide[NM + 1] + wide[NM + 2] + 6.0)
    source = wide[NM + 1][None] * grown
    fields = grown * wide[NM][None]
    for sweep in range(SWEEPS):
        lo, hi = sweep + 1, total - 1 - sweep
        beside_all = fields[:, 2:] + fields[:, :-2] + plane_around(fields[:, 1:-1])
        fields = inverse[None, lo:hi] * (source[:, lo:hi] + beside_all)
    return fields


def advance_kernel(adj_ref, left_ref, right_ref, cx_ref, cy_ref, cz_ref, coll_ref, fluid_ref, weigh_ref,
                   star_ref, part_ref):
    step = pl.program_id(0)
    g = adj_ref[...].astype(jnp.float32)
    rows, lanes = g.shape
    cx = cx_ref[...]
    cy = cy_ref[...]
    cz = cz_ref[...]
    half = NV1 // 2
    blank = jnp.zeros((rows // NV1, half, PLANE), jnp.float32)
    left = left_ref[...].astype(jnp.float32).reshape(rows // NV1, half, PLANE)
    right = right_ref[...].astype(jnp.float32).reshape(rows // NV1, half, PLANE)
    left = jnp.concatenate([left, blank], axis=1).reshape(rows, PLANE)
    right = jnp.concatenate([blank, right], axis=1).reshape(rows, PLANE)
    after = jnp.concatenate([g[:, PLANE:], right], axis=1)
    before = jnp.concatenate([left, g[:, : lanes - PLANE]], axis=1)
    lane = lax.broadcasted_iota(jnp.int32, (1, lanes), 1)
    zpos = lane % NZ
    ypos = (lane // NZ) % (PLANE // NZ)
    y_next = jnp.where(ypos == PLANE // NZ - 1, 0.0, pltpu.roll(g, lanes - NZ, 1))
    y_prev = jnp.where(ypos == 0, 0.0, pltpu.roll(g, NZ, 1))
    z_next = jnp.where(zpos == NZ - 1, 0.0, pltpu.roll(g, lanes - 1, 1))
    z_prev = jnp.where(zpos == 0, 0.0, pltpu.roll(g, 1, 1))
    term_x = jnp.maximum(cx, 0.0) * (after - g) + jnp.minimum(cx, 0.0) * (g - before)
    term_y = jnp.maximum(cy, 0.0) * (y_next - g) + jnp.minimum(cy, 0.0) * (g - y_prev)
    term_z = jnp.maximum(cz, 0.0) * (z_next - g) + jnp.minimum(cz, 0.0) * (g - z_prev)
    advect = term_x + term_y + term_z
    starred = (fluid_ref[...] * (g + TIME_STEP * (advect - coll_ref[...] * g))).astype(jnp.bfloat16)
    star_ref[...] = starred
    partial = jnp.dot(weigh_ref[...], starred, preferred_element_type=jnp.float32)

    @pl.when(step == 0)
    def _():
        part_ref[...] = partial

    @pl.when(step > 0)
    def _():
        part_ref[...] += partial


def advance(adj, left, right, cx, cy, cz, coll, fluid, weigh, block=256):
    nv, lanes = adj.shape
    nm = weigh.shape[0]
    grid = (nv // block,)
    row = lambda i: (i, 0)
    fixed = lambda i: (0, 0)
    return pl.pallas_call(
        advance_kernel,
        grid=grid,
        in_specs=[
            pl.BlockSpec((block, lanes), row),
            pl.BlockSpec((block // 2, PLANE), row),
            pl.BlockSpec((block // 2, PLANE), row),
            pl.BlockSpec((block, 1), row),
            pl.BlockSpec((block, 1), row),
            pl.BlockSpec((block, 1), row),
            pl.BlockSpec((1, lanes), fixed),
            pl.BlockSpec((1, lanes), fixed),
            pl.BlockSpec((nm, block), lambda i: (0, i)),
        ],
        out_specs=[pl.BlockSpec((block, lanes), row), pl.BlockSpec((nm, lanes), fixed)],
        out_shape=[jax.ShapeDtypeStruct((nv, lanes), jnp.bfloat16), jax.ShapeDtypeStruct((nm, lanes), jnp.float32)],
        compiler_params=pltpu.CompilerParams(dimension_semantics=("arbitrary",)),
    )(adj, left, right, cx, cy, cz, coll, fluid, weigh)


def on_device(adjoint, collision, solid, codes):
    local_vel, width, plane = adjoint.shape
    start = lax.axis_index("vel") * local_vel
    speed_x, speed_y, speed_z, weigh, lift = tables(start, local_vel)
    count = lax.axis_size("space")
    ends = count - 1
    flat = lax.optimization_barrier(adjoint.reshape(local_vel, width * plane))
    grouped = flat.reshape(local_vel // NV1, NV1, width * plane)
    half = NV1 // 2
    tail = grouped[:, :half, (width - 1) * plane :].reshape(local_vel // 2, plane)
    head = grouped[:, half:, :plane].reshape(local_vel // 2, plane)
    left = lax.ppermute(tail, "space", [(i, i + 1) for i in range(ends)])
    right = lax.ppermute(head, "space", [(i + 1, i) for i in range(ends)])
    fluid = (1 - solid).astype(jnp.float32)
    starred_flat, partial_value = advance(
        flat,
        left,
        right,
        speed_x.reshape(local_vel, 1),
        speed_y.reshape(local_vel, 1),
        speed_z.reshape(local_vel, 1),
        collision.reshape(1, width * plane),
        fluid.reshape(1, width * plane),
        weigh,
    )
    moments = lax.psum(partial_value, "vel").reshape(NM, width, plane)
    cells_all = width * lax.axis_size("space") * plane
    squares = exchange_sum(jnp.sum(moments[0] * moments[0]), "space")
    scale = lax.rsqrt(squares / cells_all + 1e-06)
    fields = sweep_all(moments, fluid, collision, wall_level(codes))
    delta = ((fields - moments) * scale).astype(jnp.bfloat16).reshape(NM, width * plane)
    lifted = lift.astype(jnp.float32).reshape(local_vel, NM, 1, 1)
    spread = delta.astype(jnp.float32).reshape(NM, width, plane)
    added = lifted[:, 0] * spread[0]
    for m in range(1, NM):
        added = added + lifted[:, m] * spread[m]
    starred_cells = starred_flat.reshape(local_vel, width, plane)
    corrected = (fluid[None] * (starred_cells + added)).astype(jnp.bfloat16)
    return (corrected, fields * scale)


def solution(mesh):
    return jax.shard_map(
        on_device,
        mesh=mesh,
        in_specs=(P("vel", "space", None), P("space", None), P("space", None), P("space", None)),
        out_specs=(P("vel", "space", None), P(None, "space", None)),
        check_vma=False,
    )
```

```python
import math

import jax
import jax.numpy as jnp
from jax import lax
from jax.sharding import PartitionSpec as P
from jax.experimental import pallas as pl
from jax.experimental.pallas import tpu as pltpu

NV1 = 16
NM = 13
NY = 16
NZ = 16
SWEEPS = 3
SPACE_AXES = ("sz", "sy", "sx")
SPACE_SIZES = (8, 4, 4)


TIME_STEP = 0.06
PLANE = NY * NZ


def with_halo(cells, sides, width):
    for axis, dim in sides:
        count = lax.axis_size(axis)
        ends = count - 1
        head = lax.slice_in_dim(cells, 0, width, axis=dim)
        tail = lax.slice_in_dim(cells, cells.shape[dim] - width, cells.shape[dim], axis=dim)
        cells = jnp.concatenate(
            [
                lax.ppermute(tail, axis, [(i, (i + 1) % count) for i in range(ends)]),
                cells,
                lax.ppermute(head, axis, [((i + 1) % count, i) for i in range(ends)]),
            ],
            axis=dim,
        )
    return cells


def exchange_sum(value, axis):
    count = lax.axis_size(axis)
    if count & (count - 1):
        return lax.psum(value, axis)
    step = 1
    while step < count:
        value = value + lax.ppermute(value, axis, [(i, i ^ step) for i in range(count)])
        step *= 2
    return value


def velocity_axes(start, count):
    index = start + jnp.arange(count, dtype=jnp.int32)
    spacing = 9.0 / NV1
    centre = (NV1 - 1) / 2.0
    along_x = ((index % NV1).astype(jnp.float32) - centre) * spacing
    along_z = ((index // NV1 % NV1).astype(jnp.float32) - centre) * spacing
    along_y = ((index // (NV1 * NV1)).astype(jnp.float32) - centre) * spacing
    return (along_x, along_y, along_z)


def tables(start, count):
    along_x, along_y, along_z = velocity_axes(start, count)
    speed = along_x * along_x + along_y * along_y + along_z * along_z
    unity = jnp.ones_like(along_x)
    basis = jnp.stack(
        [
            unity,
            along_x,
            along_y,
            along_z,
            (speed - 3.0) / math.sqrt(6.0),
            along_x * along_y,
            along_x * along_z,
            along_y * along_z,
            (along_x * along_x - along_y * along_y) / math.sqrt(2.0),
            (along_x * along_x + along_y * along_y - 2.0 * along_z * along_z) / math.sqrt(6.0),
            along_x * (speed - 5.0) / math.sqrt(10.0),
            along_y * (speed - 5.0) / math.sqrt(10.0),
            along_z * (speed - 5.0) / math.sqrt(10.0),
        ]
    )
    every_x, every_y, every_z = velocity_axes(0, NV1**3)
    total = jnp.sum(jnp.exp(-0.5 * (every_x * every_x + every_y * every_y + every_z * every_z)))
    weigh = (basis * jnp.exp(-0.5 * speed) / total).astype(jnp.bfloat16)
    lift = jnp.transpose(0.1 * basis * jnp.exp(-0.25 * speed)).astype(jnp.bfloat16)
    return (along_x, along_y, along_z, weigh, lift)


def wall_level(codes):
    return (
        0.5 * (codes == 1).astype(jnp.float32)
        + 1.5 * (codes == 2).astype(jnp.float32)
        + 4.0 * (codes == 3).astype(jnp.float32)
    )


def plane_around(fields):
    count, rows, plane = fields.shape
    cube = fields.reshape(count, rows, NY, NZ)
    padded = jnp.pad(cube, ((0, 0), (0, 0), (1, 1), (1, 1)))
    summed = (
        padded[:, :, 2:, 1:-1]
        + padded[:, :, :-2, 1:-1]
        + padded[:, :, 1:-1, 2:]
        + padded[:, :, 1:-1, :-2]
    )
    return summed.reshape(count, rows, plane)


def sweep_all(moments, fluid, collision, kappa):
    count = axis_count(SPACE_AXES)
    ends = count - 1
    width = moments.shape[1]
    depth = SWEEPS
    pack = jnp.concatenate([moments, jnp.stack([fluid, collision, kappa])], axis=0)
    before = lax.ppermute(pack[:, width - depth :], SPACE_AXES, [(i, i + 1) for i in range(ends)])
    after = lax.ppermute(pack[:, :depth], SPACE_AXES, [(i + 1, i) for i in range(ends)])
    wide = jnp.concatenate([before, pack, after], axis=1)
    total = wide.shape[1]
    grown = wide[:NM]
    inverse = wide[NM] / (wide[NM + 1] + wide[NM + 2] + 6.0)
    source = wide[NM + 1][None] * grown
    fields = grown * wide[NM][None]
    for sweep in range(SWEEPS):
        lo, hi = sweep + 1, total - 1 - sweep
        beside_all = fields[:, 2:] + fields[:, :-2] + plane_around(fields[:, 1:-1])
        fields = inverse[None, lo:hi] * (source[:, lo:hi] + beside_all)
    return fields


def advance_kernel(adj_ref, left_ref, right_ref, cx_ref, cy_ref, cz_ref, coll_ref, fluid_ref, weigh_ref,
                   star_ref, part_ref):
    step = pl.program_id(0)
    g = adj_ref[...].astype(jnp.float32)
    rows, lanes = g.shape
    cx = cx_ref[...]
    cy = cy_ref[...]
    cz = cz_ref[...]
    half = NV1 // 2
    blank = jnp.zeros((rows // NV1, half, PLANE), jnp.float32)
    left = left_ref[...].astype(jnp.float32).reshape(rows // NV1, half, PLANE)
    right = right_ref[...].astype(jnp.float32).reshape(rows // NV1, half, PLANE)
    left = jnp.concatenate([left, blank], axis=1).reshape(rows, PLANE)
    right = jnp.concatenate([blank, right], axis=1).reshape(rows, PLANE)
    after = jnp.concatenate([g[:, PLANE:], right], axis=1)
    before = jnp.concatenate([left, g[:, : lanes - PLANE]], axis=1)
    lane = lax.broadcasted_iota(jnp.int32, (1, lanes), 1)
    zpos = lane % NZ
    ypos = (lane // NZ) % (PLANE // NZ)
    y_next = jnp.where(ypos == PLANE // NZ - 1, 0.0, pltpu.roll(g, lanes - NZ, 1))
    y_prev = jnp.where(ypos == 0, 0.0, pltpu.roll(g, NZ, 1))
    z_next = jnp.where(zpos == NZ - 1, 0.0, pltpu.roll(g, lanes - 1, 1))
    z_prev = jnp.where(zpos == 0, 0.0, pltpu.roll(g, 1, 1))
    term_x = jnp.maximum(cx, 0.0) * (after - g) + jnp.minimum(cx, 0.0) * (g - before)
    term_y = jnp.maximum(cy, 0.0) * (y_next - g) + jnp.minimum(cy, 0.0) * (g - y_prev)
    term_z = jnp.maximum(cz, 0.0) * (z_next - g) + jnp.minimum(cz, 0.0) * (g - z_prev)
    advect = term_x + term_y + term_z
    starred = (fluid_ref[...] * (g + TIME_STEP * (advect - coll_ref[...] * g))).astype(jnp.bfloat16)
    star_ref[...] = starred
    partial = jnp.dot(weigh_ref[...], starred, preferred_element_type=jnp.float32)

    @pl.when(step == 0)
    def _():
        part_ref[...] = partial

    @pl.when(step > 0)
    def _():
        part_ref[...] += partial


def advance(adj, left, right, cx, cy, cz, coll, fluid, weigh, block=256):
    nv, lanes = adj.shape
    nm = weigh.shape[0]
    grid = (nv // block,)
    row = lambda i: (i, 0)
    fixed = lambda i: (0, 0)
    return pl.pallas_call(
        advance_kernel,
        grid=grid,
        in_specs=[
            pl.BlockSpec((block, lanes), row),
            pl.BlockSpec((block // 2, PLANE), row),
            pl.BlockSpec((block // 2, PLANE), row),
            pl.BlockSpec((block, 1), row),
            pl.BlockSpec((block, 1), row),
            pl.BlockSpec((block, 1), row),
            pl.BlockSpec((1, lanes), fixed),
            pl.BlockSpec((1, lanes), fixed),
            pl.BlockSpec((nm, block), lambda i: (0, i)),
        ],
        out_specs=[pl.BlockSpec((block, lanes), row), pl.BlockSpec((nm, lanes), fixed)],
        out_shape=[jax.ShapeDtypeStruct((nv, lanes), jnp.bfloat16), jax.ShapeDtypeStruct((nm, lanes), jnp.float32)],
        compiler_params=pltpu.CompilerParams(dimension_semantics=("arbitrary",)),
    )(adj, left, right, cx, cy, cz, coll, fluid, weigh)


def on_device(adjoint, collision, solid, codes):
    local_vel, width, plane = adjoint.shape
    start = lax.axis_index("vel") * local_vel
    speed_x, speed_y, speed_z, weigh, lift = tables(start, local_vel)
    count = axis_count(SPACE_AXES)
    ends = count - 1
    flat = lax.optimization_barrier(adjoint.reshape(local_vel, width * plane))
    grouped = flat.reshape(local_vel // NV1, NV1, width * plane)
    half = NV1 // 2
    tail = grouped[:, :half, (width - 1) * plane :].reshape(local_vel // 2, plane)
    head = grouped[:, half:, :plane].reshape(local_vel // 2, plane)
    left = lax.ppermute(tail, SPACE_AXES, [(i, i + 1) for i in range(ends)])
    right = lax.ppermute(head, SPACE_AXES, [(i + 1, i) for i in range(ends)])
    fluid = (1 - solid).astype(jnp.float32)
    starred_flat, partial_value = advance(
        flat,
        left,
        right,
        speed_x.reshape(local_vel, 1),
        speed_y.reshape(local_vel, 1),
        speed_z.reshape(local_vel, 1),
        collision.reshape(1, width * plane),
        fluid.reshape(1, width * plane),
        weigh,
    )
    moments = lax.psum(partial_value, "vel").reshape(NM, width, plane)
    cells_all = width * axis_count(SPACE_AXES) * plane
    squares = jnp.sum(moments[0] * moments[0])
    for axis in SPACE_AXES[::-1]:
        squares = lax.psum(squares, axis)
    scale = lax.rsqrt(squares / cells_all + 1e-06)
    fields = sweep_all(moments, fluid, collision, wall_level(codes))
    delta = ((fields - moments) * scale).astype(jnp.bfloat16).reshape(NM, width * plane)
    added = jnp.dot(lift, delta, preferred_element_type=jnp.float32)
    corrected = (fluid.reshape(1, width * plane) * (starred_flat + added)).astype(jnp.bfloat16)
    return (corrected.reshape(local_vel, width, plane), fields * scale)


def axis_count(axes):
    count = 1
    for axis in axes:
        count *= lax.axis_size(axis)
    return count


def solution(mesh):
    sizes = SPACE_SIZES if mesh.devices.shape[0] == math.prod(SPACE_SIZES) else (mesh.devices.shape[0],)
    names = SPACE_AXES if len(sizes) == len(SPACE_AXES) else ("space",)
    fine = jax.sharding.Mesh(mesh.devices.reshape(sizes + (mesh.devices.shape[1],)), names + ("vel",))
    return jax.shard_map(
        on_device,
        mesh=fine,
        in_specs=(P("vel", names, None), P(names, None), P(names, None), P(names, None)),
        out_specs=(P("vel", names, None), P(None, names, None)),
        check_vma=False,
    )
```

```python
import math

import jax
import jax.numpy as jnp
from jax import lax
from jax.sharding import PartitionSpec as P
from jax.experimental import pallas as pl
from jax.experimental.pallas import tpu as pltpu

NV1 = 16
NM = 13
NY = 16
NZ = 16
SWEEPS = 3
SPACE_AXES = ("sz", "sy", "sx")
SPACE_SIZES = (8, 4, 4)


TIME_STEP = 0.06
PLANE = NY * NZ


def with_halo(cells, sides, width):
    for axis, dim in sides:
        count = lax.axis_size(axis)
        ends = count - 1
        head = lax.slice_in_dim(cells, 0, width, axis=dim)
        tail = lax.slice_in_dim(cells, cells.shape[dim] - width, cells.shape[dim], axis=dim)
        cells = jnp.concatenate(
            [
                lax.ppermute(tail, axis, [(i, (i + 1) % count) for i in range(ends)]),
                cells,
                lax.ppermute(head, axis, [((i + 1) % count, i) for i in range(ends)]),
            ],
            axis=dim,
        )
    return cells


def exchange_sum(value, axis):
    count = lax.axis_size(axis)
    if count & (count - 1):
        return lax.psum(value, axis)
    step = 1
    while step < count:
        value = value + lax.ppermute(value, axis, [(i, i ^ step) for i in range(count)])
        step *= 2
    return value


def velocity_axes(start, count):
    index = start + jnp.arange(count, dtype=jnp.int32)
    spacing = 9.0 / NV1
    centre = (NV1 - 1) / 2.0
    along_x = ((index % NV1).astype(jnp.float32) - centre) * spacing
    along_z = ((index // NV1 % NV1).astype(jnp.float32) - centre) * spacing
    along_y = ((index // (NV1 * NV1)).astype(jnp.float32) - centre) * spacing
    return (along_x, along_y, along_z)


def tables(start, count):
    along_x, along_y, along_z = velocity_axes(start, count)
    speed = along_x * along_x + along_y * along_y + along_z * along_z
    unity = jnp.ones_like(along_x)
    basis = jnp.stack(
        [
            unity,
            along_x,
            along_y,
            along_z,
            (speed - 3.0) / math.sqrt(6.0),
            along_x * along_y,
            along_x * along_z,
            along_y * along_z,
            (along_x * along_x - along_y * along_y) / math.sqrt(2.0),
            (along_x * along_x + along_y * along_y - 2.0 * along_z * along_z) / math.sqrt(6.0),
            along_x * (speed - 5.0) / math.sqrt(10.0),
            along_y * (speed - 5.0) / math.sqrt(10.0),
            along_z * (speed - 5.0) / math.sqrt(10.0),
        ]
    )
    every_x, every_y, every_z = velocity_axes(0, NV1**3)
    total = jnp.sum(jnp.exp(-0.5 * (every_x * every_x + every_y * every_y + every_z * every_z)))
    weigh = (basis * jnp.exp(-0.5 * speed) / total).astype(jnp.bfloat16)
    lift = jnp.transpose(0.1 * basis * jnp.exp(-0.25 * speed)).astype(jnp.bfloat16)
    return (along_x, along_y, along_z, weigh, lift)


def wall_level(codes):
    return (
        0.5 * (codes == 1).astype(jnp.float32)
        + 1.5 * (codes == 2).astype(jnp.float32)
        + 4.0 * (codes == 3).astype(jnp.float32)
    )


def plane_around(fields):
    count, rows, plane = fields.shape
    cube = fields.reshape(count, rows, NY, NZ)
    padded = jnp.pad(cube, ((0, 0), (0, 0), (1, 1), (1, 1)))
    summed = (
        padded[:, :, 2:, 1:-1]
        + padded[:, :, :-2, 1:-1]
        + padded[:, :, 1:-1, 2:]
        + padded[:, :, 1:-1, :-2]
    )
    return summed.reshape(count, rows, plane)


def sweep_all(moments, fluid, collision, kappa):
    count = axis_count(SPACE_AXES)
    ends = count - 1
    width = moments.shape[1]
    depth = SWEEPS
    pack = jnp.concatenate([moments, jnp.stack([fluid, collision, kappa])], axis=0)
    before = lax.ppermute(pack[:, width - depth :], SPACE_AXES, [(i, i + 1) for i in range(ends)])
    after = lax.ppermute(pack[:, :depth], SPACE_AXES, [(i + 1, i) for i in range(ends)])
    wide = jnp.concatenate([before, pack, after], axis=1)
    total = wide.shape[1]
    grown = wide[:NM]
    inverse = wide[NM] / (wide[NM + 1] + wide[NM + 2] + 6.0)
    source = wide[NM + 1][None] * grown
    fields = grown * wide[NM][None]
    for sweep in range(SWEEPS):
        lo, hi = sweep + 1, total - 1 - sweep
        beside_all = fields[:, 2:] + fields[:, :-2] + plane_around(fields[:, 1:-1])
        fields = inverse[None, lo:hi] * (source[:, lo:hi] + beside_all)
    return fields


def advance_kernel(adj_ref, left_ref, right_ref, cy_ref, coll_ref, fluid_ref, weigh_ref,
                   star_ref, part_ref):
    step = pl.program_id(0)
    g = adj_ref[...].astype(jnp.float32)
    rows, lanes = g.shape
    spacing = 9.0 / NV1
    centre = (NV1 - 1) / 2.0
    row = step * rows + lax.broadcasted_iota(jnp.int32, (rows, 1), 0)
    cx = ((row % NV1).astype(jnp.float32) - centre) * spacing
    cz = ((row // NV1 % NV1).astype(jnp.float32) - centre) * spacing
    cy = cy_ref[...]
    half = NV1 // 2
    blank = jnp.zeros((rows // NV1, half, PLANE), jnp.float32)
    left = left_ref[...].astype(jnp.float32).reshape(rows // NV1, half, PLANE)
    right = right_ref[...].astype(jnp.float32).reshape(rows // NV1, half, PLANE)
    left = jnp.concatenate([left, blank], axis=1).reshape(rows, PLANE)
    right = jnp.concatenate([blank, right], axis=1).reshape(rows, PLANE)
    after = jnp.concatenate([g[:, PLANE:], right], axis=1)
    before = jnp.concatenate([left, g[:, : lanes - PLANE]], axis=1)
    lane = lax.broadcasted_iota(jnp.int32, (1, lanes), 1)
    zpos = lane % NZ
    ypos = (lane // NZ) % (PLANE // NZ)
    y_next = jnp.where(ypos == PLANE // NZ - 1, 0.0, pltpu.roll(g, lanes - NZ, 1))
    y_prev = jnp.where(ypos == 0, 0.0, pltpu.roll(g, NZ, 1))
    z_next = jnp.where(zpos == NZ - 1, 0.0, pltpu.roll(g, lanes - 1, 1))
    z_prev = jnp.where(zpos == 0, 0.0, pltpu.roll(g, 1, 1))
    term_x = jnp.abs(cx) * (jnp.where(cx > 0.0, after, before) - g)
    term_y = jnp.abs(cy) * (jnp.where(cy > 0.0, y_next, y_prev) - g)
    term_z = jnp.abs(cz) * (jnp.where(cz > 0.0, z_next, z_prev) - g)
    advect = term_x + term_y + term_z
    starred = (fluid_ref[...] * (g + TIME_STEP * (advect - coll_ref[...] * g))).astype(jnp.bfloat16)
    star_ref[...] = starred
    partial = jnp.dot(weigh_ref[...], starred, preferred_element_type=jnp.float32)

    @pl.when(step == 0)
    def _():
        part_ref[...] = partial

    @pl.when(step > 0)
    def _():
        part_ref[...] += partial


def advance(adj, left, right, cy, coll, fluid, weigh, block=256):
    nv, lanes = adj.shape
    nm = weigh.shape[0]
    grid = (nv // block,)
    row = lambda i: (i, 0)
    fixed = lambda i: (0, 0)
    return pl.pallas_call(
        advance_kernel,
        grid=grid,
        in_specs=[
            pl.BlockSpec((block, lanes), row),
            pl.BlockSpec((block // 2, PLANE), row),
            pl.BlockSpec((block // 2, PLANE), row),
            pl.BlockSpec((block, 1), row),
            pl.BlockSpec((1, lanes), fixed),
            pl.BlockSpec((1, lanes), fixed),
            pl.BlockSpec((nm, block), lambda i: (0, i)),
        ],
        out_specs=[pl.BlockSpec((block, lanes), row), pl.BlockSpec((nm, lanes), fixed)],
        out_shape=[jax.ShapeDtypeStruct((nv, lanes), jnp.bfloat16), jax.ShapeDtypeStruct((nm, lanes), jnp.float32)],
        compiler_params=pltpu.CompilerParams(dimension_semantics=("arbitrary",)),
    )(adj, left, right, cy, coll, fluid, weigh)


def on_device(adjoint, collision, solid, codes):
    local_vel, width, plane = adjoint.shape
    start = lax.axis_index("vel") * local_vel
    speed_x, speed_y, speed_z, weigh, lift = tables(start, local_vel)
    count = axis_count(SPACE_AXES)
    ends = count - 1
    flat = lax.optimization_barrier(adjoint.reshape(local_vel, width * plane))
    grouped = flat.reshape(local_vel // NV1, NV1, width * plane)
    half = NV1 // 2
    tail = grouped[:, :half, (width - 1) * plane :].reshape(local_vel // 2, plane)
    head = grouped[:, half:, :plane].reshape(local_vel // 2, plane)
    left = lax.ppermute(tail, SPACE_AXES, [(i, i + 1) for i in range(ends)])
    right = lax.ppermute(head, SPACE_AXES, [(i + 1, i) for i in range(ends)])
    fluid = (1 - solid).astype(jnp.float32)
    starred_flat, partial_value = advance(
        flat,
        left,
        right,
        speed_y.reshape(local_vel, 1),
        collision.reshape(1, width * plane),
        fluid.reshape(1, width * plane),
        weigh,
    )
    moments = lax.psum(partial_value, "vel").reshape(NM, width, plane)
    cells_all = width * axis_count(SPACE_AXES) * plane
    squares = jnp.sum(moments[0] * moments[0])
    for axis in SPACE_AXES[::-1]:
        squares = lax.psum(squares, axis)
    scale = lax.rsqrt(squares / cells_all + 1e-06)
    fields = sweep_all(moments, fluid, collision, wall_level(codes))
    delta = ((fields - moments) * scale).astype(jnp.bfloat16).reshape(NM, width * plane)
    added = jnp.dot(lift, delta, preferred_element_type=jnp.float32)
    corrected = (fluid.reshape(1, width * plane) * (starred_flat + added)).astype(jnp.bfloat16)
    return (corrected.reshape(local_vel, width, plane), fields * scale)


def axis_count(axes):
    count = 1
    for axis in axes:
        count *= lax.axis_size(axis)
    return count


def solution(mesh):
    sizes = SPACE_SIZES if mesh.devices.shape[0] == math.prod(SPACE_SIZES) else (mesh.devices.shape[0],)
    names = SPACE_AXES if len(sizes) == len(SPACE_AXES) else ("space",)
    fine = jax.sharding.Mesh(mesh.devices.reshape(sizes + (mesh.devices.shape[1],)), names + ("vel",))
    return jax.shard_map(
        on_device,
        mesh=fine,
        in_specs=(P("vel", names, None), P(names, None), P(names, None), P(names, None)),
        out_specs=(P("vel", names, None), P(None, names, None)),
        check_vma=False,
    )
```

```python
import math

import jax
import jax.numpy as jnp
from jax import lax
from jax.sharding import PartitionSpec as P
from jax.experimental import pallas as pl
from jax.experimental.pallas import tpu as pltpu

NV1 = 16
NM = 13
NY = 16
NZ = 16
SWEEPS = 3
SPACE_AXES = ("sz", "sy", "sx")
SPACE_SIZES = (8, 4, 4)


TIME_STEP = 0.06
PLANE = NY * NZ


def with_halo(cells, sides, width):
    for axis, dim in sides:
        count = lax.axis_size(axis)
        ends = count - 1
        head = lax.slice_in_dim(cells, 0, width, axis=dim)
        tail = lax.slice_in_dim(cells, cells.shape[dim] - width, cells.shape[dim], axis=dim)
        cells = jnp.concatenate(
            [
                lax.ppermute(tail, axis, [(i, (i + 1) % count) for i in range(ends)]),
                cells,
                lax.ppermute(head, axis, [((i + 1) % count, i) for i in range(ends)]),
            ],
            axis=dim,
        )
    return cells


def exchange_sum(value, axis):
    count = lax.axis_size(axis)
    if count & (count - 1):
        return lax.psum(value, axis)
    step = 1
    while step < count:
        value = value + lax.ppermute(value, axis, [(i, i ^ step) for i in range(count)])
        step *= 2
    return value


def velocity_axes(start, count):
    index = start + jnp.arange(count, dtype=jnp.int32)
    spacing = 9.0 / NV1
    centre = (NV1 - 1) / 2.0
    along_x = ((index % NV1).astype(jnp.float32) - centre) * spacing
    along_z = ((index // NV1 % NV1).astype(jnp.float32) - centre) * spacing
    along_y = ((index // (NV1 * NV1)).astype(jnp.float32) - centre) * spacing
    return (along_x, along_y, along_z)


def tables(start, count):
    along_x, along_y, along_z = velocity_axes(start, count)
    speed = along_x * along_x + along_y * along_y + along_z * along_z
    unity = jnp.ones_like(along_x)
    basis = jnp.stack(
        [
            unity,
            along_x,
            along_y,
            along_z,
            (speed - 3.0) / math.sqrt(6.0),
            along_x * along_y,
            along_x * along_z,
            along_y * along_z,
            (along_x * along_x - along_y * along_y) / math.sqrt(2.0),
            (along_x * along_x + along_y * along_y - 2.0 * along_z * along_z) / math.sqrt(6.0),
            along_x * (speed - 5.0) / math.sqrt(10.0),
            along_y * (speed - 5.0) / math.sqrt(10.0),
            along_z * (speed - 5.0) / math.sqrt(10.0),
        ]
    )
    every_x, every_y, every_z = velocity_axes(0, NV1**3)
    total = jnp.sum(jnp.exp(-0.5 * (every_x * every_x + every_y * every_y + every_z * every_z)))
    weigh = (basis * jnp.exp(-0.5 * speed) / total).astype(jnp.bfloat16)
    lift = jnp.transpose(0.1 * basis * jnp.exp(-0.25 * speed)).astype(jnp.bfloat16)
    return (along_x, along_y, along_z, weigh, lift)


def wall_level(codes):
    return (
        0.5 * (codes == 1).astype(jnp.float32)
        + 1.5 * (codes == 2).astype(jnp.float32)
        + 4.0 * (codes == 3).astype(jnp.float32)
    )


def plane_around(fields):
    count, rows, plane = fields.shape
    cube = fields.reshape(count, rows, NY, NZ)
    padded = jnp.pad(cube, ((0, 0), (0, 0), (1, 1), (1, 1)))
    summed = (
        padded[:, :, 2:, 1:-1]
        + padded[:, :, :-2, 1:-1]
        + padded[:, :, 1:-1, 2:]
        + padded[:, :, 1:-1, :-2]
    )
    return summed.reshape(count, rows, plane)


def sweep_all(moments, fluid, collision, kappa):
    count = axis_count(SPACE_AXES)
    ends = count - 1
    width = moments.shape[1]
    depth = SWEEPS
    pack = jnp.concatenate([moments, jnp.stack([fluid, collision, kappa])], axis=0)
    before = lax.ppermute(pack[:, width - depth :], SPACE_AXES, [(i, i + 1) for i in range(ends)])
    after = lax.ppermute(pack[:, :depth], SPACE_AXES, [(i + 1, i) for i in range(ends)])
    wide = jnp.concatenate([before, pack, after], axis=1)
    total = wide.shape[1]
    grown = wide[:NM]
    inverse = wide[NM] / (wide[NM + 1] + wide[NM + 2] + 6.0)
    source = wide[NM + 1][None] * grown
    fields = grown * wide[NM][None]
    for sweep in range(SWEEPS):
        lo, hi = sweep + 1, total - 1 - sweep
        beside_all = fields[:, 2:] + fields[:, :-2] + plane_around(fields[:, 1:-1])
        fields = inverse[None, lo:hi] * (source[:, lo:hi] + beside_all)
    return fields


def advance_kernel(adj_ref, left_ref, right_ref, cy_ref, coll_ref, fluid_ref, weigh_ref,
                   star_ref, part_ref):
    step = pl.program_id(0)
    g = adj_ref[...].astype(jnp.float32)
    rows, lanes = g.shape
    spacing = 9.0 / NV1
    centre = (NV1 - 1) / 2.0
    row = step * rows + lax.broadcasted_iota(jnp.int32, (rows, 1), 0)
    cx = ((row % NV1).astype(jnp.float32) - centre) * spacing
    cz = ((row // NV1 % NV1).astype(jnp.float32) - centre) * spacing
    cy = cy_ref[...]
    half = NV1 // 2
    blank = jnp.zeros((rows // NV1, half, PLANE), jnp.float32)
    left = left_ref[...].astype(jnp.float32).reshape(rows // NV1, half, PLANE)
    right = right_ref[...].astype(jnp.float32).reshape(rows // NV1, half, PLANE)
    left = jnp.concatenate([left, blank], axis=1).reshape(rows, PLANE)
    right = jnp.concatenate([blank, right], axis=1).reshape(rows, PLANE)
    after = jnp.concatenate([g[:, PLANE:], right], axis=1)
    before = jnp.concatenate([left, g[:, : lanes - PLANE]], axis=1)
    lane = lax.broadcasted_iota(jnp.int32, (1, lanes), 1)
    zpos = lane % NZ
    ypos = (lane // NZ) % (PLANE // NZ)
    y_next = jnp.where(ypos == PLANE // NZ - 1, 0.0, pltpu.roll(g, lanes - NZ, 1))
    y_prev = jnp.where(ypos == 0, 0.0, pltpu.roll(g, NZ, 1))
    z_next = jnp.where(zpos == NZ - 1, 0.0, pltpu.roll(g, lanes - 1, 1))
    z_prev = jnp.where(zpos == 0, 0.0, pltpu.roll(g, 1, 1))
    term_x = jnp.abs(cx) * (jnp.where(cx > 0.0, after, before) - g)
    term_y = jnp.abs(cy) * (jnp.where(cy > 0.0, y_next, y_prev) - g)
    term_z = jnp.abs(cz) * (jnp.where(cz > 0.0, z_next, z_prev) - g)
    advect = term_x + term_y + term_z
    starred = (fluid_ref[...] * (g + TIME_STEP * (advect - coll_ref[...] * g))).astype(jnp.bfloat16)
    star_ref[...] = starred
    partial = jnp.dot(weigh_ref[...], starred, preferred_element_type=jnp.float32)

    @pl.when(step == 0)
    def _():
        part_ref[...] = partial

    @pl.when(step > 0)
    def _():
        part_ref[...] += partial


def advance(adj, left, right, cy, coll, fluid, weigh, block=128):
    nv, lanes = adj.shape
    nm = weigh.shape[0]
    grid = (nv // block,)
    row = lambda i: (i, 0)
    fixed = lambda i: (0, 0)
    return pl.pallas_call(
        advance_kernel,
        grid=grid,
        in_specs=[
            pl.BlockSpec((block, lanes), row),
            pl.BlockSpec((block // 2, PLANE), row),
            pl.BlockSpec((block // 2, PLANE), row),
            pl.BlockSpec((block, 1), row),
            pl.BlockSpec((1, lanes), fixed),
            pl.BlockSpec((1, lanes), fixed),
            pl.BlockSpec((nm, block), lambda i: (0, i)),
        ],
        out_specs=[pl.BlockSpec((block, lanes), row), pl.BlockSpec((nm, lanes), fixed)],
        out_shape=[jax.ShapeDtypeStruct((nv, lanes), jnp.bfloat16), jax.ShapeDtypeStruct((nm, lanes), jnp.float32)],
        compiler_params=pltpu.CompilerParams(dimension_semantics=("arbitrary",)),
    )(adj, left, right, cy, coll, fluid, weigh)


def on_device(adjoint, collision, solid, codes):
    local_vel, width, plane = adjoint.shape
    start = lax.axis_index("vel") * local_vel
    speed_x, speed_y, speed_z, weigh, lift = tables(start, local_vel)
    count = axis_count(SPACE_AXES)
    ends = count - 1
    flat = lax.optimization_barrier(adjoint.reshape(local_vel, width * plane))
    grouped = flat.reshape(local_vel // NV1, NV1, width * plane)
    half = NV1 // 2
    tail = grouped[:, :half, (width - 1) * plane :].reshape(local_vel // 2, plane)
    head = grouped[:, half:, :plane].reshape(local_vel // 2, plane)
    left = lax.ppermute(tail, SPACE_AXES, [(i, i + 1) for i in range(ends)])
    right = lax.ppermute(head, SPACE_AXES, [(i + 1, i) for i in range(ends)])
    fluid = (1 - solid).astype(jnp.float32)
    starred_flat, partial_value = advance(
        flat,
        left,
        right,
        speed_y.reshape(local_vel, 1),
        collision.reshape(1, width * plane),
        fluid.reshape(1, width * plane),
        weigh,
    )
    moments = lax.psum(partial_value, "vel").reshape(NM, width, plane)
    cells_all = width * axis_count(SPACE_AXES) * plane
    squares = jnp.sum(moments[0] * moments[0])
    for axis in SPACE_AXES[::-1]:
        squares = lax.psum(squares, axis)
    scale = lax.rsqrt(squares / cells_all + 1e-06)
    fields = sweep_all(moments, fluid, collision, wall_level(codes))
    delta = ((fields - moments) * scale).astype(jnp.bfloat16).reshape(NM, width * plane)
    added = jnp.dot(lift, delta, preferred_element_type=jnp.float32)
    corrected = (fluid.reshape(1, width * plane) * (starred_flat + added)).astype(jnp.bfloat16)
    return (corrected.reshape(local_vel, width, plane), fields * scale)


def axis_count(axes):
    count = 1
    for axis in axes:
        count *= lax.axis_size(axis)
    return count


def solution(mesh):
    sizes = SPACE_SIZES if mesh.devices.shape[0] == math.prod(SPACE_SIZES) else (mesh.devices.shape[0],)
    names = SPACE_AXES if len(sizes) == len(SPACE_AXES) else ("space",)
    fine = jax.sharding.Mesh(mesh.devices.reshape(sizes + (mesh.devices.shape[1],)), names + ("vel",))
    return jax.shard_map(
        on_device,
        mesh=fine,
        in_specs=(P("vel", names, None), P(names, None), P(names, None), P(names, None)),
        out_specs=(P("vel", names, None), P(None, names, None)),
        check_vma=False,
    )
```

```python
import math

import jax
import jax.numpy as jnp
from jax import lax
from jax.sharding import PartitionSpec as P
from jax.experimental import pallas as pl
from jax.experimental.pallas import tpu as pltpu

NV1 = 16
NM = 13
NY = 16
NZ = 16
SWEEPS = 3
SPACE_AXES = ("sz", "sy", "sx")
SPACE_SIZES = (8, 4, 4)


TIME_STEP = 0.06
PLANE = NY * NZ


def with_halo(cells, sides, width):
    for axis, dim in sides:
        count = lax.axis_size(axis)
        ends = count - 1
        head = lax.slice_in_dim(cells, 0, width, axis=dim)
        tail = lax.slice_in_dim(cells, cells.shape[dim] - width, cells.shape[dim], axis=dim)
        cells = jnp.concatenate(
            [
                lax.ppermute(tail, axis, [(i, (i + 1) % count) for i in range(ends)]),
                cells,
                lax.ppermute(head, axis, [((i + 1) % count, i) for i in range(ends)]),
            ],
            axis=dim,
        )
    return cells


def exchange_sum(value, axis):
    count = lax.axis_size(axis)
    if count & (count - 1):
        return lax.psum(value, axis)
    step = 1
    while step < count:
        value = value + lax.ppermute(value, axis, [(i, i ^ step) for i in range(count)])
        step *= 2
    return value


def velocity_axes(start, count):
    index = start + jnp.arange(count, dtype=jnp.int32)
    spacing = 9.0 / NV1
    centre = (NV1 - 1) / 2.0
    along_x = ((index % NV1).astype(jnp.float32) - centre) * spacing
    along_z = ((index // NV1 % NV1).astype(jnp.float32) - centre) * spacing
    along_y = ((index // (NV1 * NV1)).astype(jnp.float32) - centre) * spacing
    return (along_x, along_y, along_z)


def tables(start, count):
    along_x, along_y, along_z = velocity_axes(start, count)
    speed = along_x * along_x + along_y * along_y + along_z * along_z
    unity = jnp.ones_like(along_x)
    basis = jnp.stack(
        [
            unity,
            along_x,
            along_y,
            along_z,
            (speed - 3.0) / math.sqrt(6.0),
            along_x * along_y,
            along_x * along_z,
            along_y * along_z,
            (along_x * along_x - along_y * along_y) / math.sqrt(2.0),
            (along_x * along_x + along_y * along_y - 2.0 * along_z * along_z) / math.sqrt(6.0),
            along_x * (speed - 5.0) / math.sqrt(10.0),
            along_y * (speed - 5.0) / math.sqrt(10.0),
            along_z * (speed - 5.0) / math.sqrt(10.0),
        ]
    )
    every_x, every_y, every_z = velocity_axes(0, NV1**3)
    total = jnp.sum(jnp.exp(-0.5 * (every_x * every_x + every_y * every_y + every_z * every_z)))
    weigh = (basis * jnp.exp(-0.5 * speed) / total).astype(jnp.bfloat16)
    lift = jnp.transpose(0.1 * basis * jnp.exp(-0.25 * speed)).astype(jnp.bfloat16)
    return (along_x, along_y, along_z, weigh, lift)


def wall_level(codes):
    return (
        0.5 * (codes == 1).astype(jnp.float32)
        + 1.5 * (codes == 2).astype(jnp.float32)
        + 4.0 * (codes == 3).astype(jnp.float32)
    )


def plane_around(fields):
    count, rows, plane = fields.shape
    cube = fields.reshape(count, rows, NY, NZ)
    padded = jnp.pad(cube, ((0, 0), (0, 0), (1, 1), (1, 1)))
    summed = (
        padded[:, :, 2:, 1:-1]
        + padded[:, :, :-2, 1:-1]
        + padded[:, :, 1:-1, 2:]
        + padded[:, :, 1:-1, :-2]
    )
    return summed.reshape(count, rows, plane)


def sweep_all(moments, fluid, collision, kappa):
    count = axis_count(SPACE_AXES)
    ends = count - 1
    width = moments.shape[1]
    depth = SWEEPS
    pack = jnp.concatenate([moments, jnp.stack([fluid, collision, kappa])], axis=0)
    before = lax.ppermute(pack[:, width - depth :], SPACE_AXES, [(i, i + 1) for i in range(ends)])
    after = lax.ppermute(pack[:, :depth], SPACE_AXES, [(i + 1, i) for i in range(ends)])
    wide = jnp.concatenate([before, pack, after], axis=1)
    total = wide.shape[1]
    grown = wide[:NM]
    inverse = wide[NM] / (wide[NM + 1] + wide[NM + 2] + 6.0)
    source = wide[NM + 1][None] * grown
    fields = grown * wide[NM][None]
    for sweep in range(SWEEPS):
        lo, hi = sweep + 1, total - 1 - sweep
        beside_all = fields[:, 2:] + fields[:, :-2] + plane_around(fields[:, 1:-1])
        fields = inverse[None, lo:hi] * (source[:, lo:hi] + beside_all)
    return fields


def advance_kernel(adj_ref, left_ref, right_ref, cx_ref, cy_ref, cz_ref, coll_ref, fluid_ref, weigh_ref,
                   star_ref, part_ref):
    step = pl.program_id(0)
    g = adj_ref[...].astype(jnp.float32)
    rows, lanes = g.shape
    cx = cx_ref[...]
    cy = cy_ref[...]
    cz = cz_ref[...]
    half = NV1 // 2
    blank = jnp.zeros((rows // NV1, half, PLANE), jnp.float32)
    left = left_ref[...].astype(jnp.float32).reshape(rows // NV1, half, PLANE)
    right = right_ref[...].astype(jnp.float32).reshape(rows // NV1, half, PLANE)
    left = jnp.concatenate([left, blank], axis=1).reshape(rows, PLANE)
    right = jnp.concatenate([blank, right], axis=1).reshape(rows, PLANE)
    after = jnp.concatenate([g[:, PLANE:], right], axis=1)
    before = jnp.concatenate([left, g[:, : lanes - PLANE]], axis=1)
    lane = lax.broadcasted_iota(jnp.int32, (1, lanes), 1)
    zpos = lane % NZ
    ypos = (lane // NZ) % (PLANE // NZ)
    y_next = jnp.where(ypos == PLANE // NZ - 1, 0.0, pltpu.roll(g, lanes - NZ, 1))
    y_prev = jnp.where(ypos == 0, 0.0, pltpu.roll(g, NZ, 1))
    z_next = jnp.where(zpos == NZ - 1, 0.0, pltpu.roll(g, lanes - 1, 1))
    z_prev = jnp.where(zpos == 0, 0.0, pltpu.roll(g, 1, 1))
    term_x = jnp.maximum(cx, 0.0) * (after - g) + jnp.minimum(cx, 0.0) * (g - before)
    term_y = jnp.maximum(cy, 0.0) * (y_next - g) + jnp.minimum(cy, 0.0) * (g - y_prev)
    term_z = jnp.maximum(cz, 0.0) * (z_next - g) + jnp.minimum(cz, 0.0) * (g - z_prev)
    advect = term_x + term_y + term_z
    starred = (fluid_ref[...] * (g + TIME_STEP * (advect - coll_ref[...] * g))).astype(jnp.bfloat16)
    star_ref[...] = starred
    partial = jnp.dot(weigh_ref[...], starred, preferred_element_type=jnp.float32)

    @pl.when(step == 0)
    def _():
        part_ref[...] = partial

    @pl.when(step > 0)
    def _():
        part_ref[...] += partial


def advance(adj, left, right, cx, cy, cz, coll, fluid, weigh, block=256):
    nv, lanes = adj.shape
    nm = weigh.shape[0]
    grid = (nv // block,)
    row = lambda i: (i, 0)
    fixed = lambda i: (0, 0)
    return pl.pallas_call(
        advance_kernel,
        grid=grid,
        in_specs=[
            pl.BlockSpec((block, lanes), row),
            pl.BlockSpec((block // 2, PLANE), row),
            pl.BlockSpec((block // 2, PLANE), row),
            pl.BlockSpec((block, 1), row),
            pl.BlockSpec((block, 1), row),
            pl.BlockSpec((block, 1), row),
            pl.BlockSpec((1, lanes), fixed),
            pl.BlockSpec((1, lanes), fixed),
            pl.BlockSpec((nm, block), lambda i: (0, i)),
        ],
        out_specs=[pl.BlockSpec((block, lanes), row), pl.BlockSpec((nm, lanes), fixed)],
        out_shape=[jax.ShapeDtypeStruct((nv, lanes), jnp.bfloat16), jax.ShapeDtypeStruct((nm, lanes), jnp.float32)],
        compiler_params=pltpu.CompilerParams(dimension_semantics=("arbitrary",)),
    )(adj, left, right, cx, cy, cz, coll, fluid, weigh)


def correct_kernel(star_ref, lift_ref, delta_ref, fluid_ref, out_ref):
    added = jnp.dot(lift_ref[...], delta_ref[...], preferred_element_type=jnp.float32)
    corrected = (fluid_ref[...] * (star_ref[...].astype(jnp.float32) + added)).astype(jnp.bfloat16)
    for x in range(out_ref.shape[1]):
        out_ref[:, x, :] = corrected[:, x * PLANE : (x + 1) * PLANE]


def correct(starred, lift, delta, fluid, width, block=256):
    nv, lanes = starred.shape
    nm = lift.shape[1]
    row = lambda i: (i, 0)
    fixed = lambda i: (0, 0)
    return pl.pallas_call(
        correct_kernel,
        grid=(nv // block,),
        in_specs=[
            pl.BlockSpec((block, lanes), row),
            pl.BlockSpec((block, nm), row),
            pl.BlockSpec((nm, lanes), fixed),
            pl.BlockSpec((1, lanes), fixed),
        ],
        out_specs=pl.BlockSpec((block, width, PLANE), lambda i: (i, 0, 0)),
        out_shape=jax.ShapeDtypeStruct((nv, width, PLANE), jnp.bfloat16),
        compiler_params=pltpu.CompilerParams(dimension_semantics=("arbitrary",)),
    )(starred, lift, delta, fluid)


def on_device(adjoint, collision, solid, codes):
    local_vel, width, plane = adjoint.shape
    start = lax.axis_index("vel") * local_vel
    speed_x, speed_y, speed_z, weigh, lift = tables(start, local_vel)
    count = axis_count(SPACE_AXES)
    ends = count - 1
    flat = lax.optimization_barrier(adjoint.reshape(local_vel, width * plane))
    grouped = flat.reshape(local_vel // NV1, NV1, width * plane)
    half = NV1 // 2
    tail = grouped[:, :half, (width - 1) * plane :].reshape(local_vel // 2, plane)
    head = grouped[:, half:, :plane].reshape(local_vel // 2, plane)
    left = lax.ppermute(tail, SPACE_AXES, [(i, i + 1) for i in range(ends)])
    right = lax.ppermute(head, SPACE_AXES, [(i + 1, i) for i in range(ends)])
    fluid = (1 - solid).astype(jnp.float32)
    starred_flat, partial_value = advance(
        flat,
        left,
        right,
        speed_x.reshape(local_vel, 1),
        speed_y.reshape(local_vel, 1),
        speed_z.reshape(local_vel, 1),
        collision.reshape(1, width * plane),
        fluid.reshape(1, width * plane),
        weigh,
    )
    moments = lax.psum(partial_value, "vel").reshape(NM, width, plane)
    cells_all = width * axis_count(SPACE_AXES) * plane
    squares = jnp.sum(moments[0] * moments[0])
    for axis in SPACE_AXES[::-1]:
        squares = lax.psum(squares, axis)
    scale = lax.rsqrt(squares / cells_all + 1e-06)
    fields = sweep_all(moments, fluid, collision, wall_level(codes))
    delta = ((fields - moments) * scale).astype(jnp.bfloat16).reshape(NM, width * plane)
    corrected = correct(starred_flat, lift, delta, fluid.reshape(1, width * plane), width)
    return (corrected, fields * scale)


def axis_count(axes):
    count = 1
    for axis in axes:
        count *= lax.axis_size(axis)
    return count


def solution(mesh):
    sizes = SPACE_SIZES if mesh.devices.shape[0] == math.prod(SPACE_SIZES) else (mesh.devices.shape[0],)
    names = SPACE_AXES if len(sizes) == len(SPACE_AXES) else ("space",)
    fine = jax.sharding.Mesh(mesh.devices.reshape(sizes + (mesh.devices.shape[1],)), names + ("vel",))
    return jax.shard_map(
        on_device,
        mesh=fine,
        in_specs=(P("vel", names, None), P(names, None), P(names, None), P(names, None)),
        out_specs=(P("vel", names, None), P(None, names, None)),
        check_vma=False,
    )
```

```python
import math

import jax
import jax.numpy as jnp
from jax import lax
from jax.sharding import PartitionSpec as P
from jax.experimental import pallas as pl
from jax.experimental.pallas import tpu as pltpu

NV1 = 16
NM = 13
NY = 16
NZ = 16
SWEEPS = 3
SPACE_AXES = ("sz", "sy", "sx")
SPACE_SIZES = (8, 4, 4)


TIME_STEP = 0.06
PLANE = NY * NZ


def with_halo(cells, sides, width):
    for axis, dim in sides:
        count = lax.axis_size(axis)
        ends = count - 1
        head = lax.slice_in_dim(cells, 0, width, axis=dim)
        tail = lax.slice_in_dim(cells, cells.shape[dim] - width, cells.shape[dim], axis=dim)
        cells = jnp.concatenate(
            [
                lax.ppermute(tail, axis, [(i, (i + 1) % count) for i in range(ends)]),
                cells,
                lax.ppermute(head, axis, [((i + 1) % count, i) for i in range(ends)]),
            ],
            axis=dim,
        )
    return cells


def exchange_sum(value, axis):
    count = lax.axis_size(axis)
    if count & (count - 1):
        return lax.psum(value, axis)
    step = 1
    while step < count:
        value = value + lax.ppermute(value, axis, [(i, i ^ step) for i in range(count)])
        step *= 2
    return value


def velocity_axes(start, count):
    index = start + jnp.arange(count, dtype=jnp.int32)
    spacing = 9.0 / NV1
    centre = (NV1 - 1) / 2.0
    along_x = ((index % NV1).astype(jnp.float32) - centre) * spacing
    along_z = ((index // NV1 % NV1).astype(jnp.float32) - centre) * spacing
    along_y = ((index // (NV1 * NV1)).astype(jnp.float32) - centre) * spacing
    return (along_x, along_y, along_z)


def tables(start, count):
    along_x, along_y, along_z = velocity_axes(start, count)
    speed = along_x * along_x + along_y * along_y + along_z * along_z
    unity = jnp.ones_like(along_x)
    basis = jnp.stack(
        [
            unity,
            along_x,
            along_y,
            along_z,
            (speed - 3.0) / math.sqrt(6.0),
            along_x * along_y,
            along_x * along_z,
            along_y * along_z,
            (along_x * along_x - along_y * along_y) / math.sqrt(2.0),
            (along_x * along_x + along_y * along_y - 2.0 * along_z * along_z) / math.sqrt(6.0),
            along_x * (speed - 5.0) / math.sqrt(10.0),
            along_y * (speed - 5.0) / math.sqrt(10.0),
            along_z * (speed - 5.0) / math.sqrt(10.0),
        ]
    )
    every_x, every_y, every_z = velocity_axes(0, NV1**3)
    total = jnp.sum(jnp.exp(-0.5 * (every_x * every_x + every_y * every_y + every_z * every_z)))
    weigh = (basis * jnp.exp(-0.5 * speed) / total).astype(jnp.bfloat16)
    lift = jnp.transpose(0.1 * basis * jnp.exp(-0.25 * speed)).astype(jnp.bfloat16)
    return (along_x, along_y, along_z, weigh, lift)


def wall_level(codes):
    return (
        0.5 * (codes == 1).astype(jnp.float32)
        + 1.5 * (codes == 2).astype(jnp.float32)
        + 4.0 * (codes == 3).astype(jnp.float32)
    )


def plane_around(fields):
    count, rows, plane = fields.shape
    cube = fields.reshape(count, rows, NY, NZ)
    padded = jnp.pad(cube, ((0, 0), (0, 0), (1, 1), (1, 1)))
    summed = (
        padded[:, :, 2:, 1:-1]
        + padded[:, :, :-2, 1:-1]
        + padded[:, :, 1:-1, 2:]
        + padded[:, :, 1:-1, :-2]
    )
    return summed.reshape(count, rows, plane)


def sweep_all(moments, fluid, collision, kappa):
    count = axis_count(SPACE_AXES)
    ends = count - 1
    width = moments.shape[1]
    depth = SWEEPS
    pack = jnp.concatenate([moments, jnp.stack([fluid, collision, kappa])], axis=0)
    before = lax.ppermute(pack[:, width - depth :], SPACE_AXES, [(i, i + 1) for i in range(ends)])
    after = lax.ppermute(pack[:, :depth], SPACE_AXES, [(i + 1, i) for i in range(ends)])
    wide = jnp.concatenate([before, pack, after], axis=1)
    total = wide.shape[1]
    grown = wide[:NM]
    inverse = wide[NM] / (wide[NM + 1] + wide[NM + 2] + 6.0)
    source = wide[NM + 1][None] * grown
    fields = grown * wide[NM][None]
    for sweep in range(SWEEPS):
        lo, hi = sweep + 1, total - 1 - sweep
        beside_all = fields[:, 2:] + fields[:, :-2] + plane_around(fields[:, 1:-1])
        fields = inverse[None, lo:hi] * (source[:, lo:hi] + beside_all)
    return fields


def advance_kernel(adj_ref, left_ref, right_ref, cx_ref, cy_ref, cz_ref, coll_ref, fluid_ref, weigh_ref,
                   star_ref, part_ref):
    step = pl.program_id(0)
    g = adj_ref[...].astype(jnp.float32)
    rows, lanes = g.shape
    cx = cx_ref[...]
    cy = cy_ref[...]
    cz = cz_ref[...]
    half = NV1 // 2
    blank = jnp.zeros((rows // NV1, half, PLANE), jnp.float32)
    left = left_ref[...].astype(jnp.float32).reshape(rows // NV1, half, PLANE)
    right = right_ref[...].astype(jnp.float32).reshape(rows // NV1, half, PLANE)
    left = jnp.concatenate([left, blank], axis=1).reshape(rows, PLANE)
    right = jnp.concatenate([blank, right], axis=1).reshape(rows, PLANE)
    after = jnp.concatenate([g[:, PLANE:], right], axis=1)
    before = jnp.concatenate([left, g[:, : lanes - PLANE]], axis=1)
    lane = lax.broadcasted_iota(jnp.int32, (1, lanes), 1)
    zpos = lane % NZ
    ypos = (lane // NZ) % (PLANE // NZ)
    y_next = jnp.where(ypos == PLANE // NZ - 1, 0.0, pltpu.roll(g, lanes - NZ, 1))
    y_prev = jnp.where(ypos == 0, 0.0, pltpu.roll(g, NZ, 1))
    z_next = jnp.where(zpos == NZ - 1, 0.0, pltpu.roll(g, lanes - 1, 1))
    z_prev = jnp.where(zpos == 0, 0.0, pltpu.roll(g, 1, 1))
    term_x = jnp.maximum(cx, 0.0) * (after - g) + jnp.minimum(cx, 0.0) * (g - before)
    term_y = jnp.maximum(cy, 0.0) * (y_next - g) + jnp.minimum(cy, 0.0) * (g - y_prev)
    term_z = jnp.maximum(cz, 0.0) * (z_next - g) + jnp.minimum(cz, 0.0) * (g - z_prev)
    advect = term_x + term_y + term_z
    starred = (fluid_ref[...] * (g + TIME_STEP * (advect - coll_ref[...] * g))).astype(jnp.bfloat16)
    star_ref[...] = starred
    partial = jnp.dot(weigh_ref[...], starred, preferred_element_type=jnp.float32)

    @pl.when(step == 0)
    def _():
        part_ref[...] = partial

    @pl.when(step > 0)
    def _():
        part_ref[...] += partial


def advance(adj, left, right, cx, cy, cz, coll, fluid, weigh, block=256):
    nv, lanes = adj.shape
    nm = weigh.shape[0]
    grid = (nv // block,)
    row = lambda i: (i, 0)
    fixed = lambda i: (0, 0)
    return pl.pallas_call(
        advance_kernel,
        grid=grid,
        in_specs=[
            pl.BlockSpec((block, lanes), row),
            pl.BlockSpec((block // 2, PLANE), row),
            pl.BlockSpec((block // 2, PLANE), row),
            pl.BlockSpec((block, 1), row),
            pl.BlockSpec((block, 1), row),
            pl.BlockSpec((block, 1), row),
            pl.BlockSpec((1, lanes), fixed),
            pl.BlockSpec((1, lanes), fixed),
            pl.BlockSpec((nm, block), lambda i: (0, i)),
        ],
        out_specs=[pl.BlockSpec((block, lanes), row), pl.BlockSpec((nm, lanes), fixed)],
        out_shape=[jax.ShapeDtypeStruct((nv, lanes), jnp.bfloat16), jax.ShapeDtypeStruct((nm, lanes), jnp.float32)],
        compiler_params=pltpu.CompilerParams(dimension_semantics=("arbitrary",)),
    )(adj, left, right, cx, cy, cz, coll, fluid, weigh)


def correct_kernel(star_ref, lift_ref, delta_ref, fluid_ref, out_ref):
    added = jnp.dot(lift_ref[...], delta_ref[...], preferred_element_type=jnp.float32)
    corrected = (fluid_ref[...] * (star_ref[...].astype(jnp.float32) + added)).astype(jnp.bfloat16)
    for x in range(out_ref.shape[1]):
        out_ref[:, x, :] = corrected[:, x * PLANE : (x + 1) * PLANE]


def correct(starred, lift, delta, fluid, width, block=256):
    nv, lanes = starred.shape
    nm = lift.shape[1]
    row = lambda i: (i, 0)
    fixed = lambda i: (0, 0)
    return pl.pallas_call(
        correct_kernel,
        grid=(nv // block,),
        in_specs=[
            pl.BlockSpec((block, lanes), row),
            pl.BlockSpec((block, nm), row),
            pl.BlockSpec((nm, lanes), fixed),
            pl.BlockSpec((1, lanes), fixed),
        ],
        out_specs=pl.BlockSpec((block, width, PLANE), lambda i: (i, 0, 0)),
        out_shape=jax.ShapeDtypeStruct((nv, width, PLANE), jnp.bfloat16),
        compiler_params=pltpu.CompilerParams(dimension_semantics=("arbitrary",)),
    )(starred, lift, delta, fluid)


def on_device(adjoint, collision, solid, codes):
    local_vel, width, plane = adjoint.shape
    start = lax.axis_index("vel") * local_vel
    every = tables(0, NV1**3)
    speed_x, speed_y, speed_z, lift = (
        lax.dynamic_slice_in_dim(table, start, local_vel, 0) for table in (every[0], every[1], every[2], every[4])
    )
    weigh = lax.dynamic_slice_in_dim(every[3], start, local_vel, 1)
    count = axis_count(SPACE_AXES)
    ends = count - 1
    flat = lax.optimization_barrier(adjoint.reshape(local_vel, width * plane))
    grouped = flat.reshape(local_vel // NV1, NV1, width * plane)
    half = NV1 // 2
    tail = grouped[:, :half, (width - 1) * plane :].reshape(local_vel // 2, plane)
    head = grouped[:, half:, :plane].reshape(local_vel // 2, plane)
    left = lax.ppermute(tail, SPACE_AXES, [(i, i + 1) for i in range(ends)])
    right = lax.ppermute(head, SPACE_AXES, [(i + 1, i) for i in range(ends)])
    fluid = (1 - solid).astype(jnp.float32)
    starred_flat, partial_value = advance(
        flat,
        left,
        right,
        speed_x.reshape(local_vel, 1),
        speed_y.reshape(local_vel, 1),
        speed_z.reshape(local_vel, 1),
        collision.reshape(1, width * plane),
        fluid.reshape(1, width * plane),
        weigh,
    )
    moments = lax.psum(partial_value, "vel").reshape(NM, width, plane)
    cells_all = width * axis_count(SPACE_AXES) * plane
    squares = jnp.sum(moments[0] * moments[0])
    for axis in SPACE_AXES[::-1]:
        squares = lax.psum(squares, axis)
    scale = lax.rsqrt(squares / cells_all + 1e-06)
    fields = sweep_all(moments, fluid, collision, wall_level(codes))
    delta = ((fields - moments) * scale).astype(jnp.bfloat16).reshape(NM, width * plane)
    corrected = correct(starred_flat, lift, delta, fluid.reshape(1, width * plane), width)
    return (corrected, fields * scale)


def axis_count(axes):
    count = 1
    for axis in axes:
        count *= lax.axis_size(axis)
    return count


def solution(mesh):
    sizes = SPACE_SIZES if mesh.devices.shape[0] == math.prod(SPACE_SIZES) else (mesh.devices.shape[0],)
    names = SPACE_AXES if len(sizes) == len(SPACE_AXES) else ("space",)
    fine = jax.sharding.Mesh(mesh.devices.reshape(sizes + (mesh.devices.shape[1],)), names + ("vel",))
    return jax.shard_map(
        on_device,
        mesh=fine,
        in_specs=(P("vel", names, None), P(names, None), P(names, None), P(names, None)),
        out_specs=(P("vel", names, None), P(None, names, None)),
        check_vma=False,
    )
```

```python
import math

import jax
import jax.numpy as jnp
from jax import lax
from jax.sharding import PartitionSpec as P
from jax.experimental import pallas as pl
from jax.experimental.pallas import tpu as pltpu

NV1 = 16
NM = 13
NY = 16
NZ = 16
SWEEPS = 3
SPACE_AXES = ("sz", "sy", "sx")
SPACE_SIZES = (8, 4, 4)


TIME_STEP = 0.06
PLANE = NY * NZ


def with_halo(cells, sides, width):
    for axis, dim in sides:
        count = lax.axis_size(axis)
        ends = count - 1
        head = lax.slice_in_dim(cells, 0, width, axis=dim)
        tail = lax.slice_in_dim(cells, cells.shape[dim] - width, cells.shape[dim], axis=dim)
        cells = jnp.concatenate(
            [
                lax.ppermute(tail, axis, [(i, (i + 1) % count) for i in range(ends)]),
                cells,
                lax.ppermute(head, axis, [((i + 1) % count, i) for i in range(ends)]),
            ],
            axis=dim,
        )
    return cells


def exchange_sum(value, axis):
    count = lax.axis_size(axis)
    if count & (count - 1):
        return lax.psum(value, axis)
    step = 1
    while step < count:
        value = value + lax.ppermute(value, axis, [(i, i ^ step) for i in range(count)])
        step *= 2
    return value


def velocity_axes(start, count):
    index = start + jnp.arange(count, dtype=jnp.int32)
    spacing = 9.0 / NV1
    centre = (NV1 - 1) / 2.0
    along_x = ((index % NV1).astype(jnp.float32) - centre) * spacing
    along_z = ((index // NV1 % NV1).astype(jnp.float32) - centre) * spacing
    along_y = ((index // (NV1 * NV1)).astype(jnp.float32) - centre) * spacing
    return (along_x, along_y, along_z)


def tables(start, count):
    along_x, along_y, along_z = velocity_axes(start, count)
    speed = along_x * along_x + along_y * along_y + along_z * along_z
    unity = jnp.ones_like(along_x)
    basis = jnp.stack(
        [
            unity,
            along_x,
            along_y,
            along_z,
            (speed - 3.0) / math.sqrt(6.0),
            along_x * along_y,
            along_x * along_z,
            along_y * along_z,
            (along_x * along_x - along_y * along_y) / math.sqrt(2.0),
            (along_x * along_x + along_y * along_y - 2.0 * along_z * along_z) / math.sqrt(6.0),
            along_x * (speed - 5.0) / math.sqrt(10.0),
            along_y * (speed - 5.0) / math.sqrt(10.0),
            along_z * (speed - 5.0) / math.sqrt(10.0),
        ]
    )
    every_x, every_y, every_z = velocity_axes(0, NV1**3)
    total = jnp.sum(jnp.exp(-0.5 * (every_x * every_x + every_y * every_y + every_z * every_z)))
    weigh = (basis * jnp.exp(-0.5 * speed) / total).astype(jnp.bfloat16)
    lift = jnp.transpose(0.1 * basis * jnp.exp(-0.25 * speed)).astype(jnp.bfloat16)
    return (along_x, along_y, along_z, weigh, lift)


def wall_level(codes):
    return (
        0.5 * (codes == 1).astype(jnp.float32)
        + 1.5 * (codes == 2).astype(jnp.float32)
        + 4.0 * (codes == 3).astype(jnp.float32)
    )


def plane_around(fields):
    count, rows, plane = fields.shape
    cube = fields.reshape(count, rows, NY, NZ)
    padded = jnp.pad(cube, ((0, 0), (0, 0), (1, 1), (1, 1)))
    summed = (
        padded[:, :, 2:, 1:-1]
        + padded[:, :, :-2, 1:-1]
        + padded[:, :, 1:-1, 2:]
        + padded[:, :, 1:-1, :-2]
    )
    return summed.reshape(count, rows, plane)


def sweep_all(moments, fluid, collision, kappa):
    count = axis_count(SPACE_AXES)
    ends = count - 1
    width = moments.shape[1]
    depth = SWEEPS
    pack = jnp.concatenate([moments, jnp.stack([fluid, collision, kappa])], axis=0)
    before = lax.ppermute(pack[:, width - depth :], SPACE_AXES, [(i, i + 1) for i in range(ends)])
    after = lax.ppermute(pack[:, :depth], SPACE_AXES, [(i + 1, i) for i in range(ends)])
    wide = jnp.concatenate([before, pack, after], axis=1)
    total = wide.shape[1]
    grown = wide[:NM]
    inverse = wide[NM] / (wide[NM + 1] + wide[NM + 2] + 6.0)
    source = wide[NM + 1][None] * grown
    fields = grown * wide[NM][None]
    for sweep in range(SWEEPS):
        lo, hi = sweep + 1, total - 1 - sweep
        beside_all = fields[:, 2:] + fields[:, :-2] + plane_around(fields[:, 1:-1])
        fields = inverse[None, lo:hi] * (source[:, lo:hi] + beside_all)
    return fields


def advance_kernel(adj_ref, left_ref, right_ref, cx_ref, cy_ref, cz_ref, coll_ref, fluid_ref, weigh_ref,
                   star_ref, part_ref):
    step = pl.program_id(0)
    g = adj_ref[...].astype(jnp.float32)
    rows, lanes = g.shape
    cx = cx_ref[...]
    cy = cy_ref[...]
    cz = cz_ref[...]
    half = NV1 // 2
    blank = jnp.zeros((rows // NV1, half, PLANE), jnp.float32)
    left = left_ref[...].astype(jnp.float32).reshape(rows // NV1, half, PLANE)
    right = right_ref[...].astype(jnp.float32).reshape(rows // NV1, half, PLANE)
    left = jnp.concatenate([left, blank], axis=1).reshape(rows, PLANE)
    right = jnp.concatenate([blank, right], axis=1).reshape(rows, PLANE)
    after = jnp.concatenate([g[:, PLANE:], right], axis=1)
    before = jnp.concatenate([left, g[:, : lanes - PLANE]], axis=1)
    lane = lax.broadcasted_iota(jnp.int32, (1, lanes), 1)
    zpos = lane % NZ
    ypos = (lane // NZ) % (PLANE // NZ)
    y_next = jnp.where(ypos == PLANE // NZ - 1, 0.0, pltpu.roll(g, lanes - NZ, 1))
    y_prev = jnp.where(ypos == 0, 0.0, pltpu.roll(g, NZ, 1))
    z_next = jnp.where(zpos == NZ - 1, 0.0, pltpu.roll(g, lanes - 1, 1))
    z_prev = jnp.where(zpos == 0, 0.0, pltpu.roll(g, 1, 1))
    term_x = jnp.maximum(cx, 0.0) * (after - g) + jnp.minimum(cx, 0.0) * (g - before)
    term_y = jnp.maximum(cy, 0.0) * (y_next - g) + jnp.minimum(cy, 0.0) * (g - y_prev)
    term_z = jnp.maximum(cz, 0.0) * (z_next - g) + jnp.minimum(cz, 0.0) * (g - z_prev)
    advect = term_x + term_y + term_z
    starred = (fluid_ref[...] * (g + TIME_STEP * (advect - coll_ref[...] * g))).astype(jnp.bfloat16)
    star_ref[...] = starred
    partial = jnp.dot(weigh_ref[...], starred, preferred_element_type=jnp.float32)

    @pl.when(step == 0)
    def _():
        part_ref[...] = partial

    @pl.when(step > 0)
    def _():
        part_ref[...] += partial


def advance(adj, left, right, cx, cy, cz, coll, fluid, weigh, block=256):
    nv, lanes = adj.shape
    nm = weigh.shape[0]
    grid = (nv // block,)
    row = lambda i: (i, 0)
    fixed = lambda i: (0, 0)
    return pl.pallas_call(
        advance_kernel,
        grid=grid,
        in_specs=[
            pl.BlockSpec((block, lanes), row),
            pl.BlockSpec((block // 2, PLANE), row),
            pl.BlockSpec((block // 2, PLANE), row),
            pl.BlockSpec((block, 1), row),
            pl.BlockSpec((block, 1), row),
            pl.BlockSpec((block, 1), row),
            pl.BlockSpec((1, lanes), fixed),
            pl.BlockSpec((1, lanes), fixed),
            pl.BlockSpec((nm, block), lambda i: (0, i)),
        ],
        out_specs=[pl.BlockSpec((block, lanes), row), pl.BlockSpec((nm, lanes), fixed)],
        out_shape=[jax.ShapeDtypeStruct((nv, lanes), jnp.bfloat16), jax.ShapeDtypeStruct((nm, lanes), jnp.float32)],
        compiler_params=pltpu.CompilerParams(dimension_semantics=("arbitrary",)),
    )(adj, left, right, cx, cy, cz, coll, fluid, weigh)


def correct_kernel(star_ref, lift_ref, delta_ref, fluid_ref, out_ref):
    added = jnp.dot(lift_ref[...], delta_ref[...], preferred_element_type=jnp.float32)
    corrected = (fluid_ref[...] * (star_ref[...].astype(jnp.float32) + added)).astype(jnp.bfloat16)
    for x in range(out_ref.shape[1]):
        out_ref[:, x, :] = corrected[:, x * PLANE : (x + 1) * PLANE]


def correct(starred, lift, delta, fluid, width, block=256):
    nv, lanes = starred.shape
    nm = lift.shape[1]
    row = lambda i: (i, 0)
    fixed = lambda i: (0, 0)
    return pl.pallas_call(
        correct_kernel,
        grid=(nv // block,),
        in_specs=[
            pl.BlockSpec((block, lanes), row),
            pl.BlockSpec((block, nm), row),
            pl.BlockSpec((nm, lanes), fixed),
            pl.BlockSpec((1, lanes), fixed),
        ],
        out_specs=pl.BlockSpec((block, width, PLANE), lambda i: (i, 0, 0)),
        out_shape=jax.ShapeDtypeStruct((nv, width, PLANE), jnp.bfloat16),
        compiler_params=pltpu.CompilerParams(dimension_semantics=("arbitrary",)),
    )(starred, lift, delta, fluid)


def on_device(adjoint, collision, solid, codes):
    local_vel, width, plane = adjoint.shape
    start = lax.axis_index("vel") * local_vel
    every = tables(0, NV1**3)
    speed_x, speed_y, speed_z, lift = (
        lax.dynamic_slice_in_dim(table, start, local_vel, 0) for table in (every[0], every[1], every[2], every[4])
    )
    weigh = lax.dynamic_slice_in_dim(every[3], start, local_vel, 1)
    count = axis_count(SPACE_AXES)
    ends = count - 1
    flat = lax.optimization_barrier(adjoint.reshape(local_vel, width * plane))
    grouped = flat.reshape(local_vel // NV1, NV1, width * plane)
    half = NV1 // 2
    tail = grouped[:, :half, (width - 1) * plane :].reshape(local_vel // 2, plane)
    head = grouped[:, half:, :plane].reshape(local_vel // 2, plane)
    left = lax.ppermute(tail, SPACE_AXES, [(i, i + 1) for i in range(ends)])
    right = lax.ppermute(head, SPACE_AXES, [(i + 1, i) for i in range(ends)])
    fluid = (1 - solid).astype(jnp.float32)
    starred_flat, partial_value = advance(
        flat,
        left,
        right,
        speed_x.reshape(local_vel, 1),
        speed_y.reshape(local_vel, 1),
        speed_z.reshape(local_vel, 1),
        collision.reshape(1, width * plane),
        fluid.reshape(1, width * plane),
        weigh,
    )
    moments = (partial_value + lax.ppermute(partial_value, "vel", [(0, 1), (1, 0)])).reshape(NM, width, plane)
    cells_all = width * axis_count(SPACE_AXES) * plane
    squares = jnp.sum(moments[0] * moments[0])
    for axis in SPACE_AXES[::-1]:
        squares = lax.psum(squares, axis)
    scale = lax.rsqrt(squares / cells_all + 1e-06)
    fields = sweep_all(moments, fluid, collision, wall_level(codes))
    delta = ((fields - moments) * scale).astype(jnp.bfloat16).reshape(NM, width * plane)
    corrected = correct(starred_flat, lift, delta, fluid.reshape(1, width * plane), width)
    return (corrected, fields * scale)


def axis_count(axes):
    count = 1
    for axis in axes:
        count *= lax.axis_size(axis)
    return count


def solution(mesh):
    sizes = SPACE_SIZES if mesh.devices.shape[0] == math.prod(SPACE_SIZES) else (mesh.devices.shape[0],)
    names = SPACE_AXES if len(sizes) == len(SPACE_AXES) else ("space",)
    fine = jax.sharding.Mesh(mesh.devices.reshape(sizes + (mesh.devices.shape[1],)), names + ("vel",))
    return jax.shard_map(
        on_device,
        mesh=fine,
        in_specs=(P("vel", names, None), P(names, None), P(names, None), P(names, None)),
        out_specs=(P("vel", names, None), P(None, names, None)),
        check_vma=False,
    )
```

```python
import math

import jax
import jax.numpy as jnp
from jax import lax
from jax.sharding import PartitionSpec as P
from jax.experimental import pallas as pl
from jax.experimental.pallas import tpu as pltpu

NV1 = 16
NM = 13
NY = 16
NZ = 16
SWEEPS = 3
SPACE_AXES = ("sz", "sy", "sx")
SPACE_SIZES = (8, 4, 4)


TIME_STEP = 0.06
PLANE = NY * NZ


def with_halo(cells, sides, width):
    for axis, dim in sides:
        count = lax.axis_size(axis)
        ends = count - 1
        head = lax.slice_in_dim(cells, 0, width, axis=dim)
        tail = lax.slice_in_dim(cells, cells.shape[dim] - width, cells.shape[dim], axis=dim)
        cells = jnp.concatenate(
            [
                lax.ppermute(tail, axis, [(i, (i + 1) % count) for i in range(ends)]),
                cells,
                lax.ppermute(head, axis, [((i + 1) % count, i) for i in range(ends)]),
            ],
            axis=dim,
        )
    return cells


def exchange_sum(value, axis):
    count = lax.axis_size(axis)
    if count & (count - 1):
        return lax.psum(value, axis)
    step = 1
    while step < count:
        value = value + lax.ppermute(value, axis, [(i, i ^ step) for i in range(count)])
        step *= 2
    return value


def velocity_axes(start, count):
    index = start + jnp.arange(count, dtype=jnp.int32)
    spacing = 9.0 / NV1
    centre = (NV1 - 1) / 2.0
    along_x = ((index % NV1).astype(jnp.float32) - centre) * spacing
    along_z = ((index // NV1 % NV1).astype(jnp.float32) - centre) * spacing
    along_y = ((index // (NV1 * NV1)).astype(jnp.float32) - centre) * spacing
    return (along_x, along_y, along_z)


def tables(start, count):
    along_x, along_y, along_z = velocity_axes(start, count)
    speed = along_x * along_x + along_y * along_y + along_z * along_z
    unity = jnp.ones_like(along_x)
    basis = jnp.stack(
        [
            unity,
            along_x,
            along_y,
            along_z,
            (speed - 3.0) / math.sqrt(6.0),
            along_x * along_y,
            along_x * along_z,
            along_y * along_z,
            (along_x * along_x - along_y * along_y) / math.sqrt(2.0),
            (along_x * along_x + along_y * along_y - 2.0 * along_z * along_z) / math.sqrt(6.0),
            along_x * (speed - 5.0) / math.sqrt(10.0),
            along_y * (speed - 5.0) / math.sqrt(10.0),
            along_z * (speed - 5.0) / math.sqrt(10.0),
        ]
    )
    every_x, every_y, every_z = velocity_axes(0, NV1**3)
    total = jnp.sum(jnp.exp(-0.5 * (every_x * every_x + every_y * every_y + every_z * every_z)))
    weigh = (basis * jnp.exp(-0.5 * speed) / total).astype(jnp.bfloat16)
    lift = jnp.transpose(0.1 * basis * jnp.exp(-0.25 * speed)).astype(jnp.bfloat16)
    return (along_x, along_y, along_z, weigh, lift)


def wall_level(codes):
    return (
        0.5 * (codes == 1).astype(jnp.float32)
        + 1.5 * (codes == 2).astype(jnp.float32)
        + 4.0 * (codes == 3).astype(jnp.float32)
    )


def plane_around(fields):
    count, rows, plane = fields.shape
    cube = fields.reshape(count, rows, NY, NZ)
    padded = jnp.pad(cube, ((0, 0), (0, 0), (1, 1), (1, 1)))
    summed = (
        padded[:, :, 2:, 1:-1]
        + padded[:, :, :-2, 1:-1]
        + padded[:, :, 1:-1, 2:]
        + padded[:, :, 1:-1, :-2]
    )
    return summed.reshape(count, rows, plane)


def sweep_all(moments, fluid, collision, kappa):
    count = axis_count(SPACE_AXES)
    ends = count - 1
    width = moments.shape[1]
    depth = SWEEPS
    pack = jnp.concatenate([moments, jnp.stack([fluid, collision, kappa])], axis=0)
    before = lax.ppermute(pack[:, width - depth :], SPACE_AXES, [(i, i + 1) for i in range(ends)])
    after = lax.ppermute(pack[:, :depth], SPACE_AXES, [(i + 1, i) for i in range(ends)])
    wide = jnp.concatenate([before, pack, after], axis=1)
    total = wide.shape[1]
    grown = wide[:NM]
    inverse = wide[NM] / (wide[NM + 1] + wide[NM + 2] + 6.0)
    source = wide[NM + 1][None] * grown
    fields = grown * wide[NM][None]
    for sweep in range(SWEEPS):
        lo, hi = sweep + 1, total - 1 - sweep
        beside_all = fields[:, 2:] + fields[:, :-2] + plane_around(fields[:, 1:-1])
        fields = inverse[None, lo:hi] * (source[:, lo:hi] + beside_all)
    return fields


def advance_kernel(adj_ref, left_ref, right_ref, cx_ref, cy_ref, cz_ref, coll_ref, fluid_ref, weigh_ref,
                   star_ref, part_ref):
    step = pl.program_id(0)
    g = adj_ref[...].astype(jnp.float32)
    rows, lanes = g.shape
    cx = cx_ref[...]
    cy = cy_ref[...]
    cz = cz_ref[...]
    half = NV1 // 2
    blank = jnp.zeros((rows // NV1, half, PLANE), jnp.float32)
    left = left_ref[...].astype(jnp.float32).reshape(rows // NV1, half, PLANE)
    right = right_ref[...].astype(jnp.float32).reshape(rows // NV1, half, PLANE)
    left = jnp.concatenate([left, blank], axis=1).reshape(rows, PLANE)
    right = jnp.concatenate([blank, right], axis=1).reshape(rows, PLANE)
    after = jnp.concatenate([g[:, PLANE:], right], axis=1)
    before = jnp.concatenate([left, g[:, : lanes - PLANE]], axis=1)
    lane = lax.broadcasted_iota(jnp.int32, (1, lanes), 1)
    zpos = lane % NZ
    ypos = (lane // NZ) % (PLANE // NZ)
    y_next = jnp.where(ypos == PLANE // NZ - 1, 0.0, pltpu.roll(g, lanes - NZ, 1))
    y_prev = jnp.where(ypos == 0, 0.0, pltpu.roll(g, NZ, 1))
    z_next = jnp.where(zpos == NZ - 1, 0.0, pltpu.roll(g, lanes - 1, 1))
    z_prev = jnp.where(zpos == 0, 0.0, pltpu.roll(g, 1, 1))
    term_x = jnp.maximum(cx, 0.0) * (after - g) + jnp.minimum(cx, 0.0) * (g - before)
    term_y = jnp.maximum(cy, 0.0) * (y_next - g) + jnp.minimum(cy, 0.0) * (g - y_prev)
    term_z = jnp.maximum(cz, 0.0) * (z_next - g) + jnp.minimum(cz, 0.0) * (g - z_prev)
    advect = term_x + term_y + term_z
    starred = (fluid_ref[...] * (g + TIME_STEP * (advect - coll_ref[...] * g))).astype(jnp.bfloat16)
    star_ref[...] = starred
    partial = jnp.dot(weigh_ref[...], starred, preferred_element_type=jnp.float32)

    @pl.when(step == 0)
    def _():
        part_ref[...] = partial

    @pl.when(step > 0)
    def _():
        part_ref[...] += partial


def advance(adj, left, right, cx, cy, cz, coll, fluid, weigh, block=256):
    nv, lanes = adj.shape
    nm = weigh.shape[0]
    grid = (nv // block,)
    row = lambda i: (i, 0)
    fixed = lambda i: (0, 0)
    return pl.pallas_call(
        advance_kernel,
        grid=grid,
        in_specs=[
            pl.BlockSpec((block, lanes), row),
            pl.BlockSpec((block // 2, PLANE), row),
            pl.BlockSpec((block // 2, PLANE), row),
            pl.BlockSpec((block, 1), row),
            pl.BlockSpec((block, 1), row),
            pl.BlockSpec((block, 1), row),
            pl.BlockSpec((1, lanes), fixed),
            pl.BlockSpec((1, lanes), fixed),
            pl.BlockSpec((nm, block), lambda i: (0, i)),
        ],
        out_specs=[pl.BlockSpec((block, lanes), row), pl.BlockSpec((nm, lanes), fixed)],
        out_shape=[jax.ShapeDtypeStruct((nv, lanes), jnp.bfloat16), jax.ShapeDtypeStruct((nm, lanes), jnp.float32)],
        compiler_params=pltpu.CompilerParams(dimension_semantics=("arbitrary",)),
    )(adj, left, right, cx, cy, cz, coll, fluid, weigh)


def correct_kernel(star_ref, lift_ref, delta_ref, fluid_ref, out_ref):
    added = jnp.dot(lift_ref[...], delta_ref[...], preferred_element_type=jnp.float32)
    corrected = (fluid_ref[...] * (star_ref[...].astype(jnp.float32) + added)).astype(jnp.bfloat16)
    for x in range(out_ref.shape[1]):
        out_ref[:, x, :] = corrected[:, x * PLANE : (x + 1) * PLANE]


def correct(starred, lift, delta, fluid, width, block=256):
    nv, lanes = starred.shape
    nm = lift.shape[1]
    row = lambda i: (i, 0)
    fixed = lambda i: (0, 0)
    return pl.pallas_call(
        correct_kernel,
        grid=(nv // block,),
        in_specs=[
            pl.BlockSpec((block, lanes), row),
            pl.BlockSpec((block, nm), row),
            pl.BlockSpec((nm, lanes), fixed),
            pl.BlockSpec((1, lanes), fixed),
        ],
        out_specs=pl.BlockSpec((block, width, PLANE), lambda i: (i, 0, 0)),
        out_shape=jax.ShapeDtypeStruct((nv, width, PLANE), jnp.bfloat16),
        compiler_params=pltpu.CompilerParams(dimension_semantics=("arbitrary",)),
    )(starred, lift, delta, fluid)


def on_device(adjoint, collision, solid, codes):
    local_vel, width, plane = adjoint.shape
    start = lax.axis_index("vel") * local_vel
    every = tables(0, NV1**3)
    speed_x, speed_y, speed_z, lift = (
        lax.dynamic_slice_in_dim(table, start, local_vel, 0) for table in (every[0], every[1], every[2], every[4])
    )
    weigh = lax.dynamic_slice_in_dim(every[3], start, local_vel, 1)
    count = axis_count(SPACE_AXES)
    ends = count - 1
    flat = lax.optimization_barrier(adjoint.reshape(local_vel, width * plane))
    grouped = flat.reshape(local_vel // NV1, NV1, width * plane)
    half = NV1 // 2
    tail = grouped[:, :half, (width - 1) * plane :].reshape(local_vel // 2, plane)
    head = grouped[:, half:, :plane].reshape(local_vel // 2, plane)
    left = lax.ppermute(tail, SPACE_AXES, [(i, i + 1) for i in range(ends)])
    right = lax.ppermute(head, SPACE_AXES, [(i + 1, i) for i in range(ends)])
    fluid = (1 - solid).astype(jnp.float32)
    starred_flat, partial_value = advance(
        flat,
        left,
        right,
        speed_x.reshape(local_vel, 1),
        speed_y.reshape(local_vel, 1),
        speed_z.reshape(local_vel, 1),
        collision.reshape(1, width * plane),
        fluid.reshape(1, width * plane),
        weigh,
    )
    moments = (partial_value + lax.ppermute(partial_value, "vel", [(0, 1), (1, 0)])).reshape(NM, width, plane)
    cells_all = width * axis_count(SPACE_AXES) * plane
    squares = jnp.sum(moments[0] * moments[0])
    for axis in SPACE_AXES[::-1]:
        squares = exchange_sum(squares, axis) if axis == SPACE_AXES[-1] else lax.psum(squares, axis)
    scale = lax.rsqrt(squares / cells_all + 1e-06)
    fields = sweep_all(moments, fluid, collision, wall_level(codes))
    delta = ((fields - moments) * scale).astype(jnp.bfloat16).reshape(NM, width * plane)
    corrected = correct(starred_flat, lift, delta, fluid.reshape(1, width * plane), width)
    return (corrected, fields * scale)


def axis_count(axes):
    count = 1
    for axis in axes:
        count *= lax.axis_size(axis)
    return count


def solution(mesh):
    sizes = SPACE_SIZES if mesh.devices.shape[0] == math.prod(SPACE_SIZES) else (mesh.devices.shape[0],)
    names = SPACE_AXES if len(sizes) == len(SPACE_AXES) else ("space",)
    fine = jax.sharding.Mesh(mesh.devices.reshape(sizes + (mesh.devices.shape[1],)), names + ("vel",))
    return jax.shard_map(
        on_device,
        mesh=fine,
        in_specs=(P("vel", names, None), P(names, None), P(names, None), P(names, None)),
        out_specs=(P("vel", names, None), P(None, names, None)),
        check_vma=False,
    )
```

```python
import math

import jax
import jax.numpy as jnp
from jax import lax
from jax.sharding import PartitionSpec as P
from jax.experimental import pallas as pl
from jax.experimental.pallas import tpu as pltpu

NV1 = 16
NM = 13
NY = 16
NZ = 16
SWEEPS = 3
SPACE_AXES = ("sz", "sy", "sx")
SPACE_SIZES = (8, 4, 4)


TIME_STEP = 0.06
PLANE = NY * NZ


def with_halo(cells, sides, width):
    for axis, dim in sides:
        count = lax.axis_size(axis)
        ends = count - 1
        head = lax.slice_in_dim(cells, 0, width, axis=dim)
        tail = lax.slice_in_dim(cells, cells.shape[dim] - width, cells.shape[dim], axis=dim)
        cells = jnp.concatenate(
            [
                lax.ppermute(tail, axis, [(i, (i + 1) % count) for i in range(ends)]),
                cells,
                lax.ppermute(head, axis, [((i + 1) % count, i) for i in range(ends)]),
            ],
            axis=dim,
        )
    return cells


def exchange_sum(value, axis):
    count = lax.axis_size(axis)
    if count & (count - 1):
        return lax.psum(value, axis)
    step = 1
    while step < count:
        value = value + lax.ppermute(value, axis, [(i, i ^ step) for i in range(count)])
        step *= 2
    return value


def velocity_axes(start, count):
    index = start + jnp.arange(count, dtype=jnp.int32)
    spacing = 9.0 / NV1
    centre = (NV1 - 1) / 2.0
    along_x = ((index % NV1).astype(jnp.float32) - centre) * spacing
    along_z = ((index // NV1 % NV1).astype(jnp.float32) - centre) * spacing
    along_y = ((index // (NV1 * NV1)).astype(jnp.float32) - centre) * spacing
    return (along_x, along_y, along_z)


def tables(start, count):
    along_x, along_y, along_z = velocity_axes(start, count)
    speed = along_x * along_x + along_y * along_y + along_z * along_z
    unity = jnp.ones_like(along_x)
    basis = jnp.stack(
        [
            unity,
            along_x,
            along_y,
            along_z,
            (speed - 3.0) / math.sqrt(6.0),
            along_x * along_y,
            along_x * along_z,
            along_y * along_z,
            (along_x * along_x - along_y * along_y) / math.sqrt(2.0),
            (along_x * along_x + along_y * along_y - 2.0 * along_z * along_z) / math.sqrt(6.0),
            along_x * (speed - 5.0) / math.sqrt(10.0),
            along_y * (speed - 5.0) / math.sqrt(10.0),
            along_z * (speed - 5.0) / math.sqrt(10.0),
        ]
    )
    every_x, every_y, every_z = velocity_axes(0, NV1**3)
    total = jnp.sum(jnp.exp(-0.5 * (every_x * every_x + every_y * every_y + every_z * every_z)))
    weigh = (basis * jnp.exp(-0.5 * speed) / total).astype(jnp.bfloat16)
    lift = jnp.transpose(0.1 * basis * jnp.exp(-0.25 * speed)).astype(jnp.bfloat16)
    return (along_x, along_y, along_z, weigh, lift)


def wall_level(codes):
    return (
        0.5 * (codes == 1).astype(jnp.float32)
        + 1.5 * (codes == 2).astype(jnp.float32)
        + 4.0 * (codes == 3).astype(jnp.float32)
    )


def plane_around(fields):
    count, rows, plane = fields.shape
    cube = fields.reshape(count, rows, NY, NZ)
    padded = jnp.pad(cube, ((0, 0), (0, 0), (1, 1), (1, 1)))
    summed = (
        padded[:, :, 2:, 1:-1]
        + padded[:, :, :-2, 1:-1]
        + padded[:, :, 1:-1, 2:]
        + padded[:, :, 1:-1, :-2]
    )
    return summed.reshape(count, rows, plane)


def sweep_all(moments, fluid, collision, kappa):
    count = axis_count(SPACE_AXES)
    ends = count - 1
    width = moments.shape[1]
    depth = SWEEPS
    pack = jnp.concatenate([moments, jnp.stack([fluid, collision, kappa])], axis=0)
    before = lax.ppermute(pack[:, width - depth :], SPACE_AXES, [(i, i + 1) for i in range(ends)])
    after = lax.ppermute(pack[:, :depth], SPACE_AXES, [(i + 1, i) for i in range(ends)])
    wide = jnp.concatenate([before, pack, after], axis=1)
    total = wide.shape[1]
    grown = wide[:NM]
    inverse = wide[NM] / (wide[NM + 1] + wide[NM + 2] + 6.0)
    source = wide[NM + 1][None] * grown
    fields = grown * wide[NM][None]
    for sweep in range(SWEEPS):
        lo, hi = sweep + 1, total - 1 - sweep
        beside_all = fields[:, 2:] + fields[:, :-2] + plane_around(fields[:, 1:-1])
        fields = inverse[None, lo:hi] * (source[:, lo:hi] + beside_all)
    return fields


def advance_kernel(adj_ref, left_ref, right_ref, cx_ref, cy_ref, cz_ref, coll_ref, fluid_ref, weigh_ref,
                   star_ref, part_ref):
    step = pl.program_id(0)
    g = adj_ref[...].astype(jnp.float32)
    rows, lanes = g.shape
    cx = cx_ref[...]
    cy = cy_ref[...]
    cz = cz_ref[...]
    half = NV1 // 2
    blank = jnp.zeros((rows // NV1, half, PLANE), jnp.float32)
    left = left_ref[...].astype(jnp.float32).reshape(rows // NV1, half, PLANE)
    right = right_ref[...].astype(jnp.float32).reshape(rows // NV1, half, PLANE)
    left = jnp.concatenate([left, blank], axis=1).reshape(rows, PLANE)
    right = jnp.concatenate([blank, right], axis=1).reshape(rows, PLANE)
    after = jnp.concatenate([g[:, PLANE:], right], axis=1)
    before = jnp.concatenate([left, g[:, : lanes - PLANE]], axis=1)
    lane = lax.broadcasted_iota(jnp.int32, (1, lanes), 1)
    zpos = lane % NZ
    ypos = (lane // NZ) % (PLANE // NZ)
    y_next = jnp.where(ypos == PLANE // NZ - 1, 0.0, pltpu.roll(g, lanes - NZ, 1))
    y_prev = jnp.where(ypos == 0, 0.0, pltpu.roll(g, NZ, 1))
    z_next = jnp.where(zpos == NZ - 1, 0.0, pltpu.roll(g, lanes - 1, 1))
    z_prev = jnp.where(zpos == 0, 0.0, pltpu.roll(g, 1, 1))
    term_x = jnp.maximum(cx, 0.0) * (after - g) + jnp.minimum(cx, 0.0) * (g - before)
    term_y = jnp.maximum(cy, 0.0) * (y_next - g) + jnp.minimum(cy, 0.0) * (g - y_prev)
    term_z = jnp.maximum(cz, 0.0) * (z_next - g) + jnp.minimum(cz, 0.0) * (g - z_prev)
    advect = term_x + term_y + term_z
    starred = (fluid_ref[...] * (g + TIME_STEP * (advect - coll_ref[...] * g))).astype(jnp.bfloat16)
    star_ref[...] = starred
    partial = jnp.dot(weigh_ref[...], starred, preferred_element_type=jnp.float32)

    @pl.when(step == 0)
    def _():
        part_ref[...] = partial

    @pl.when(step > 0)
    def _():
        part_ref[...] += partial


def advance(adj, left, right, cx, cy, cz, coll, fluid, weigh, block=512):
    nv, lanes = adj.shape
    nm = weigh.shape[0]
    grid = (nv // block,)
    row = lambda i: (i, 0)
    fixed = lambda i: (0, 0)
    return pl.pallas_call(
        advance_kernel,
        grid=grid,
        in_specs=[
            pl.BlockSpec((block, lanes), row),
            pl.BlockSpec((block // 2, PLANE), row),
            pl.BlockSpec((block // 2, PLANE), row),
            pl.BlockSpec((block, 1), row),
            pl.BlockSpec((block, 1), row),
            pl.BlockSpec((block, 1), row),
            pl.BlockSpec((1, lanes), fixed),
            pl.BlockSpec((1, lanes), fixed),
            pl.BlockSpec((nm, block), lambda i: (0, i)),
        ],
        out_specs=[pl.BlockSpec((block, lanes), row), pl.BlockSpec((nm, lanes), fixed)],
        out_shape=[jax.ShapeDtypeStruct((nv, lanes), jnp.bfloat16), jax.ShapeDtypeStruct((nm, lanes), jnp.float32)],
        compiler_params=pltpu.CompilerParams(dimension_semantics=("arbitrary",)),
    )(adj, left, right, cx, cy, cz, coll, fluid, weigh)


def correct_kernel(star_ref, lift_ref, delta_ref, fluid_ref, out_ref):
    added = jnp.dot(lift_ref[...], delta_ref[...], preferred_element_type=jnp.float32)
    corrected = (fluid_ref[...] * (star_ref[...].astype(jnp.float32) + added)).astype(jnp.bfloat16)
    for x in range(out_ref.shape[1]):
        out_ref[:, x, :] = corrected[:, x * PLANE : (x + 1) * PLANE]


def correct(starred, lift, delta, fluid, width, block=256):
    nv, lanes = starred.shape
    nm = lift.shape[1]
    row = lambda i: (i, 0)
    fixed = lambda i: (0, 0)
    return pl.pallas_call(
        correct_kernel,
        grid=(nv // block,),
        in_specs=[
            pl.BlockSpec((block, lanes), row),
            pl.BlockSpec((block, nm), row),
            pl.BlockSpec((nm, lanes), fixed),
            pl.BlockSpec((1, lanes), fixed),
        ],
        out_specs=pl.BlockSpec((block, width, PLANE), lambda i: (i, 0, 0)),
        out_shape=jax.ShapeDtypeStruct((nv, width, PLANE), jnp.bfloat16),
        compiler_params=pltpu.CompilerParams(dimension_semantics=("arbitrary",)),
    )(starred, lift, delta, fluid)


def on_device(adjoint, collision, solid, codes):
    local_vel, width, plane = adjoint.shape
    start = lax.axis_index("vel") * local_vel
    every = tables(0, NV1**3)
    speed_x, speed_y, speed_z, lift = (
        lax.dynamic_slice_in_dim(table, start, local_vel, 0) for table in (every[0], every[1], every[2], every[4])
    )
    weigh = lax.dynamic_slice_in_dim(every[3], start, local_vel, 1)
    count = axis_count(SPACE_AXES)
    ends = count - 1
    flat = lax.optimization_barrier(adjoint.reshape(local_vel, width * plane))
    grouped = flat.reshape(local_vel // NV1, NV1, width * plane)
    half = NV1 // 2
    tail = grouped[:, :half, (width - 1) * plane :].reshape(local_vel // 2, plane)
    head = grouped[:, half:, :plane].reshape(local_vel // 2, plane)
    left = lax.ppermute(tail, SPACE_AXES, [(i, i + 1) for i in range(ends)])
    right = lax.ppermute(head, SPACE_AXES, [(i + 1, i) for i in range(ends)])
    fluid = (1 - solid).astype(jnp.float32)
    starred_flat, partial_value = advance(
        flat,
        left,
        right,
        speed_x.reshape(local_vel, 1),
        speed_y.reshape(local_vel, 1),
        speed_z.reshape(local_vel, 1),
        collision.reshape(1, width * plane),
        fluid.reshape(1, width * plane),
        weigh,
    )
    moments = (partial_value + lax.ppermute(partial_value, "vel", [(0, 1), (1, 0)])).reshape(NM, width, plane)
    cells_all = width * axis_count(SPACE_AXES) * plane
    squares = jnp.sum(moments[0] * moments[0])
    for axis in SPACE_AXES[::-1]:
        squares = lax.psum(squares, axis)
    scale = lax.rsqrt(squares / cells_all + 1e-06)
    fields = sweep_all(moments, fluid, collision, wall_level(codes))
    delta = ((fields - moments) * scale).astype(jnp.bfloat16).reshape(NM, width * plane)
    corrected = correct(starred_flat, lift, delta, fluid.reshape(1, width * plane), width)
    return (corrected, fields * scale)


def axis_count(axes):
    count = 1
    for axis in axes:
        count *= lax.axis_size(axis)
    return count


def solution(mesh):
    sizes = SPACE_SIZES if mesh.devices.shape[0] == math.prod(SPACE_SIZES) else (mesh.devices.shape[0],)
    names = SPACE_AXES if len(sizes) == len(SPACE_AXES) else ("space",)
    fine = jax.sharding.Mesh(mesh.devices.reshape(sizes + (mesh.devices.shape[1],)), names + ("vel",))
    return jax.shard_map(
        on_device,
        mesh=fine,
        in_specs=(P("vel", names, None), P(names, None), P(names, None), P(names, None)),
        out_specs=(P("vel", names, None), P(None, names, None)),
        check_vma=False,
    )
```
